32 devices in a mesh: band: 16 (over z, y, core), win: 2 (over x).
Axes of the slice: x: 2, y: 2, z: 4, core: 2. Of those that a mesh axis runs over, the one named last changes fastest.
Arguments:
- first_guess: float32 [2, 15, 128, 128], P('win', None, 'band'), may hold values from -6 to 6
- observed_height: float32 [2, 15, 128, 128], P('win', None, 'band'), may hold values from -6 to 6
- swath_cells: int32 [2, 15, 16, 256], P('win', None, 'band'), may hold values from 0 to 1023, as said below
- drift_value: float32 [2, 16, 16, 32], P('win', 'band'), may hold values from -6 to 6
- drift_cell: int32 [2, 16, 16, 32], P('win', 'band'), may hold values from -1 to 15359, as said below
- prior_in: bfloat16 [9, 64, 15], replicated, may hold values from -0.5 to 0.5
- prior_out: bfloat16 [9, 15, 64], replicated, may hold values from -0.25 to 0.25
- lstm_weight: bfloat16 [9, 143, 512], replicated, may hold values from -0.15625 to 0.15625
- lstm_bias: float32 [512], replicated, may hold values from -4 to 4
- out_weight: bfloat16 [15, 128], replicated, may hold values from -0.5 to 0.5
- final_slope: float32 [2, 15, 128, 128], P('win', None, 'band'), may hold values from -6 to 6
Outputs:
- grad_first: float32 [2, 15, 128, 128], P('win', None, 'band')
- grad_prior_in: float32 [9, 64, 15], replicated
- grad_prior_out: float32 [9, 15, 64], replicated
- grad_lstm: float32 [9, 143, 512], replicated
- grad_bias: float32 [512], replicated
- grad_out: float32 [15, 128], replicated
The draws below stay inside these ranges and needn't reach their ends.
Inputs may be any that keep to these rules, and one draw needn't show every extreme that they name: `swath_cells`: each list holds 256 different cells of one band's block in one frame, a cell numbered column * 128 + row. `drift_cell`: a record's cell in its destination band's block, numbered frame * 8 * 128 + column * 128 + row, or -1 for an empty slot; live slots come first in each list of 32; in every window some band receives 32 live records from every band.
All inputs are finite; a program needn't handle non-finite values.
Results may differ from the reference program's by a relative error of at most 0.0058.
Values may be sent and summed in bfloat16 or wider, within the bound.
No kernel may reach another device: no remote copies, remote signals or barrier semaphores. Data moves between devices by JAX's collectives and lax.ppermute only.
A program may use at most 64 MiB of HBM per device.

```python
import jax
import jax.numpy as jnp
from jax import lax

F = 15
C = 64
H = 128
BW = 8
LAT = 128
CAP = 32
BANDS = 16
NWIN = 2
NLON = 128
SW = 256


def draw_drift_cell(key, part):
    folded = jax.random.fold_in(key, 11)
    key_busy, key_count, key_cell = jax.random.split(folded, 3)
    busiest = jax.random.randint(key_busy, (NWIN,), 0, BANDS)
    counts = jax.random.randint(key_count, (NWIN, BANDS, BANDS), CAP // 8, CAP // 2 + 1)
    target = jnp.arange(BANDS)[None, None, :] == busiest[:, None, None]
    counts = jnp.where(target, CAP, counts)
    cell_ids = jax.random.randint(key_cell, (NWIN, BANDS, BANDS, CAP), 0, F * BW * LAT)
    cell_ids = cell_ids.at[:, 0, :, 0].set(F * BW * LAT - 1)
    occupied = jnp.arange(CAP)[None, None, None, :] < counts[..., None]
    return jnp.where(occupied, cell_ids, -1).astype(jnp.int32)


def draw_swath_cells(key, part):
    folded = jax.random.fold_in(key, 23)
    keyring = jax.random.split(folded, NWIN * F * BANDS)
    chosen = jax.vmap(lambda single: jax.random.permutation(single, BW * LAT)[:SW])(keyring)
    return chosen.reshape(NWIN, F, BANDS, SW).astype(jnp.int32)


def shard_levels(stream_key, extent, cuts, least, largest):
    gain = 1.0
    for dim, blocks in cuts:
        steps = jax.random.uniform(jax.random.fold_in(jax.random.fold_in(stream_key, 6), dim), (blocks,), jnp.float32, least / len(cuts), largest / len(cuts))
        gain = gain * jnp.repeat(jnp.exp(steps), extent[dim] // blocks).reshape((-1,) + (1,) * (len(extent) - 1 - dim))
    return gain


def noise(key, shape, spread, reach, cuts=(), kind=jnp.bfloat16):
    result = jax.random.normal(key, shape, jnp.float32) * spread
    if len(cuts) > 0:
        result = shard_levels(key, shape, cuts, -0.22, 0.18) * result
    return jnp.clip(result, min=-reach, max=reach).astype(kind)


def setup_inputs(seed: int = 0) -> dict:
    seeds = jax.random.split(jax.random.key(seed), 12)
    first_guess = noise(seeds[0], (NWIN, F, NLON, LAT), 1.0, 6.0, ((0, 2), (2, 16)), jnp.float32)
    observed_height = noise(seeds[1], (NWIN, F, NLON, LAT), 1.0, 6.0, ((0, 2), (2, 16)), jnp.float32)
    swath_cells = draw_swath_cells(jax.random.fold_in(seeds[11], 71), 0)
    drift_value = noise(seeds[3], (NWIN, BANDS, BANDS, CAP), 1.0, 6.0, ((0, 2), (1, 16)), jnp.float32)
    drift_cell = draw_drift_cell(jax.random.fold_in(seeds[11], 71), 0)
    prior_in = noise(seeds[5], (9, C, F), (9 * F) ** -0.5, 0.5)
    prior_out = noise(seeds[6], (9, F, C), (9 * C) ** -0.5, 0.25)
    lstm_weight = noise(seeds[7], (9, F + H, 4 * H), (9 * (F + H)) ** -0.5, 0.15625)
    lstm_bias = noise(seeds[8], (4 * H,), 1.0, 4.0, (), jnp.float32)
    out_weight = noise(seeds[9], (F, H), H ** -0.5, 0.5)
    final_slope = noise(seeds[10], (NWIN, F, NLON, LAT), 1.0, 6.0, ((0, 2), (2, 16)), jnp.float32)
    return {"first_guess": first_guess, "observed_height": observed_height, "swath_cells": swath_cells, "drift_value": drift_value, "drift_cell": drift_cell, "prior_in": prior_in, "prior_out": prior_out, "lstm_weight": lstm_weight, "lstm_bias": lstm_bias, "out_weight": out_weight, "final_slope": final_slope}


prior_weight = 1.0

def conv_three(kernel, padded, form='oi'):
    breadth = padded.shape[2] - 2
    lat_count = padded.shape[3]
    framed = jnp.pad(padded, ((0, 0), (0, 0), (0, 0), (1, 1)))
    summed = None
    for lon_off in range(3):
        for lat_off in range(3):
            window = framed[:, :, lon_off:lon_off + breadth, lat_off:lat_off + lat_count]
            contrib = jnp.einsum(form + ',biwl->bowl', kernel[3 * lon_off + lat_off].astype(jnp.float32), window.astype(jnp.float32))
            summed = contrib if summed is None else summed + contrib
    return summed

def kernel_slope(cotangent, padded, form='oi'):
    breadth = cotangent.shape[2]
    lat_count = cotangent.shape[3]
    framed = jnp.pad(padded, ((0, 0), (0, 0), (0, 0), (1, 1)))
    pieces = []
    for lon_off in range(3):
        for lat_off in range(3):
            window = framed[:, :, lon_off:lon_off + breadth, lat_off:lat_off + lat_count]
            pieces.append(jnp.einsum('bowl,biwl->' + form, cotangent.astype(jnp.float32), window.astype(jnp.float32)))
    return jnp.stack(pieces)

def flipped(kernel):
    return jnp.transpose(kernel[::-1], (0, 2, 1))

def rimmed(field):
    return jnp.pad(field, ((0, 0), (0, 0), (1, 1), (0, 0)))

def forward(current, hidden, memory, obs_weight, obs_target, weights):
    prior_in, prior_out, lstm_weight, lstm_bias, out_weight = weights
    units = out_weight.shape[1]
    state_rim = rimmed(current.astype(jnp.bfloat16))
    pre_prior = conv_three(prior_in, state_rim)
    latent = jax.nn.silu(pre_prior).astype(jnp.bfloat16)
    latent_rim = rimmed(latent)
    prior_state = conv_three(prior_out, latent_rim)
    cost_slope = obs_weight * current - obs_target + prior_weight * (current - prior_state)
    joined = jnp.concatenate([cost_slope, hidden], axis=1).astype(jnp.bfloat16)
    joined_rim = rimmed(joined)
    gate_all = conv_three(lstm_weight, joined_rim, 'io') + lstm_bias[None, :, None, None]
    in_gate = jax.nn.sigmoid(gate_all[:, :units])
    forget_gate = jax.nn.sigmoid(gate_all[:, units:2 * units])
    out_gate = jax.nn.sigmoid(gate_all[:, 2 * units:3 * units])
    update = jnp.tanh(gate_all[:, 3 * units:])
    memory_next = forget_gate * memory + in_gate * update
    squashed = jnp.tanh(memory_next)
    hidden_next = out_gate * squashed
    hidden_low = hidden_next.astype(jnp.bfloat16)
    stepped = jnp.einsum('fh,bhwl->bfwl', out_weight.astype(jnp.float32), hidden_low.astype(jnp.float32))
    saved = (state_rim, pre_prior, latent_rim, joined_rim, in_gate, forget_gate, out_gate, update, memory, squashed, hidden_low)
    return (current - stepped, hidden_next, memory_next, saved)

def backward(slope_state, slope_hidden, slope_memory, saved, obs_weight, weights, leading):
    prior_in, prior_out, lstm_weight, lstm_bias, out_weight = weights
    state_rim, pre_prior, latent_rim, joined_rim, in_gate, forget_gate, out_gate, update, memory, squashed, hidden_low = saved
    frames = slope_state.shape[1]
    neg_low = (-slope_state).astype(jnp.bfloat16)
    grad_outw = jnp.einsum('bfwl,bhwl->fh', neg_low.astype(jnp.float32), hidden_low.astype(jnp.float32))
    slope_hid = jnp.einsum('fh,bfwl->bhwl', out_weight.astype(jnp.float32), neg_low.astype(jnp.float32)) + slope_hidden
    slope_mem = slope_hid * out_gate * (1.0 - squashed * squashed) + slope_memory
    gate_slope = jnp.concatenate([slope_mem * update * in_gate * (1.0 - in_gate), slope_mem * memory * forget_gate * (1.0 - forget_gate), slope_hid * squashed * out_gate * (1.0 - out_gate), slope_mem * in_gate * (1.0 - update * update)], axis=1)
    grad_bias = lax.optimization_barrier(jnp.sum(gate_slope, axis=(0, 2, 3)))
    gate_low = gate_slope.astype(jnp.bfloat16)
    grad_lstm = kernel_slope(gate_low, joined_rim, 'io')
    back_kernel = lstm_weight[::-1]
    if leading:
        back_kernel = back_kernel[:, :frames]
    joined_slope = conv_three(back_kernel, rimmed(gate_low))
    cost_part = joined_slope[:, :frames]
    hidden_back = None if leading else joined_slope[:, frames:]
    slope_prev = slope_state + (obs_weight + prior_weight) * cost_part
    prior_low = (-prior_weight * cost_part).astype(jnp.bfloat16)
    grad_pout = kernel_slope(prior_low, latent_rim)
    latent_slope = conv_three(flipped(prior_out), rimmed(prior_low))
    sigma = jax.nn.sigmoid(pre_prior)
    pre_low = (latent_slope * (sigma + pre_prior * sigma * (1.0 - sigma))).astype(jnp.bfloat16)
    grad_pin = kernel_slope(pre_low, state_rim)
    slope_prev = slope_prev + conv_three(flipped(prior_in), rimmed(pre_low))
    memory_back = slope_mem * forget_gate
    return (slope_prev, hidden_back, memory_back, (grad_pin, grad_pout, grad_lstm, grad_bias, grad_outw))

def reference(first_guess, observed_height, swath_cells, drift_value, drift_cell, prior_in, prior_out, lstm_weight, lstm_bias, out_weight, final_slope):
    block = BW * LAT
    plane = NLON * LAT
    window_ids = jnp.arange(NWIN, dtype=jnp.int32)
    frame_ids = jnp.arange(F, dtype=jnp.int32)
    band_ids = jnp.arange(BANDS, dtype=jnp.int32)
    placed = ((window_ids[:, None, None, None] * F + frame_ids[None, :, None, None]) * plane + band_ids[None, None, :, None] * block + swath_cells).astype(jnp.int32)
    mask = jnp.zeros((NWIN * F * plane,), jnp.float32).at[placed.reshape(-1)].set(1.0).reshape(NWIN, F, NLON, LAT)
    occupied = drift_cell >= 0
    safe_cell = jnp.where(occupied, drift_cell, 0).astype(jnp.int32)
    target_idx = ((window_ids[:, None, None, None] * F + safe_cell // block) * plane + band_ids[None, None, :, None] * block + safe_cell % block).astype(jnp.int32)
    drift_count = jnp.zeros((NWIN * F * plane,), jnp.float32).at[target_idx.reshape(-1)].add(jnp.where(occupied, 1.0, 0.0).astype(jnp.float32).reshape(-1)).reshape(NWIN, F, NLON, LAT)
    drift_total = jnp.zeros((NWIN * F * plane,), jnp.float32).at[target_idx.reshape(-1)].add(jnp.where(occupied, drift_value, 0.0).astype(jnp.float32).reshape(-1)).reshape(NWIN, F, NLON, LAT)
    obs_weight = mask + drift_count
    obs_target = mask * observed_height + drift_total
    weights = (prior_in, prior_out, lstm_weight, lstm_bias, out_weight)

    def one_window(packed):
        guess, weight_one, target_one, slope_one = packed
        guess = guess[None]
        weight_one = weight_one[None]
        target_one = target_one[None]
        slope_one = slope_one[None]
        blank = jnp.zeros((1, H, NLON, LAT), jnp.float32)
        state_one, hid_one, mem_one, saved_one = forward(guess, blank, blank, weight_one, target_one, weights)
        state_two, hid_two, mem_two, saved_two = forward(state_one, hid_one, mem_one, weight_one, target_one, weights)
        slope_mid, hidden_back, memory_back, grads_two = backward(slope_one, blank, blank, saved_two, weight_one, weights, False)
        slope_start, unused_hid, unused_mem, grads_one = backward(slope_mid, hidden_back, memory_back, saved_one, weight_one, weights, True)
        return (slope_start[0], jax.tree.map(jnp.add, grads_one, grads_two))
    grad_first, stacked = lax.map(one_window, (first_guess, obs_weight, obs_target, final_slope))
    scale = 1.0 / jnp.sqrt(jnp.float32(NWIN * NLON * LAT))
    totals = [lax.optimization_barrier(jnp.sum(member, axis=0)) * scale for member in stacked]
    return (grad_first, totals[0], totals[1], totals[2], totals[3], totals[4])
```

```python
import jax
import jax.numpy as jnp
from jax import lax
from jax.sharding import PartitionSpec as P

prior_weight = 1.0


def padded_2(array, sides, width):
    for axis, dim in sides:
        size, length = (lax.axis_size(axis), array.shape[dim])
        up = [(i, (i + 1) % size) for i in range(size - 1)]
        down = [(j, i) for i, j in up]
        last = lax.slice_in_dim(array, length - width, length, axis=dim)
        first = lax.slice_in_dim(array, 0, width, axis=dim)
        before = lax.ppermute(last, axis, up)
        after = lax.ppermute(first, axis, down)
        array = jnp.concatenate([before, array, after], axis=dim)
    return array


def conv_three(kernel, padded, form="oi"):
    breadth = padded.shape[2] - 2
    lat_count = padded.shape[3]
    framed = jnp.pad(padded, ((0, 0), (0, 0), (0, 0), (1, 1)))
    summed = None
    for lon_off in range(3):
        for lat_off in range(3):
            window = framed[:, :, lon_off : lon_off + breadth, lat_off : lat_off + lat_count]
            contrib = jnp.einsum(
                form + ",biwl->bowl",
                kernel[3 * lon_off + lat_off],
                window,
                preferred_element_type=jnp.float32,
            )
            summed = contrib if summed is None else summed + contrib
    return summed


def kernel_slope(cotangent, padded, form="oi"):
    breadth = cotangent.shape[2]
    lat_count = cotangent.shape[3]
    framed = jnp.pad(padded, ((0, 0), (0, 0), (0, 0), (1, 1)))
    pieces = []
    for lon_off in range(3):
        for lat_off in range(3):
            window = framed[:, :, lon_off : lon_off + breadth, lat_off : lat_off + lat_count]
            pieces.append(
                jnp.einsum(
                    "bowl,biwl->" + form, cotangent, window, preferred_element_type=jnp.float32
                )
            )
    return jnp.stack(pieces)


def flipped(kernel):
    return jnp.transpose(kernel[::-1], (0, 2, 1))


def rimmed_field(field):
    return padded_2(field, (("band", 2),), 1)


def rimmed_slope(field):
    return padded_2(field, (("band", 2),), 1)


def forward(current, hidden, memory, obs_weight, obs_target, weights):
    prior_in, prior_out, lstm_weight, lstm_bias, out_weight = weights
    units = out_weight.shape[1]
    state_rim = rimmed_field(current.astype(jnp.bfloat16))
    pre_prior = conv_three(prior_in, state_rim)
    latent = jax.nn.silu(pre_prior).astype(jnp.bfloat16)
    latent_rim = rimmed_field(latent)
    prior_state = conv_three(prior_out, latent_rim)
    cost_slope = obs_weight * current - obs_target + prior_weight * (current - prior_state)
    joined = jnp.concatenate([cost_slope, hidden], axis=1).astype(jnp.bfloat16)
    joined_rim = rimmed_field(joined)
    gate_all = conv_three(lstm_weight, joined_rim, "io") + lstm_bias[None, :, None, None]
    in_gate = jax.nn.sigmoid(gate_all[:, :units])
    forget_gate = jax.nn.sigmoid(gate_all[:, units : 2 * units])
    out_gate = jax.nn.sigmoid(gate_all[:, 2 * units : 3 * units])
    update = jnp.tanh(gate_all[:, 3 * units :])
    memory_next = forget_gate * memory + in_gate * update
    squashed = jnp.tanh(memory_next)
    hidden_next = out_gate * squashed
    hidden_low = hidden_next.astype(jnp.bfloat16)
    stepped = jnp.einsum(
        "fh,bhwl->bfwl", out_weight, hidden_low, preferred_element_type=jnp.float32
    )
    saved = (
        state_rim,
        pre_prior,
        latent_rim,
        joined_rim,
        in_gate,
        forget_gate,
        out_gate,
        update,
        memory,
        squashed,
        hidden_low,
    )
    return (current - stepped, hidden_next, memory_next, saved)


def backward(slope_state, slope_hidden, slope_memory, saved, obs_weight, weights, leading):
    prior_in, prior_out, lstm_weight, lstm_bias, out_weight = weights
    (
        state_rim,
        pre_prior,
        latent_rim,
        joined_rim,
        in_gate,
        forget_gate,
        out_gate,
        update,
        memory,
        squashed,
        hidden_low,
    ) = saved
    frames = slope_state.shape[1]
    neg_low = (-slope_state).astype(jnp.bfloat16)
    grad_outw = jnp.einsum("bfwl,bhwl->fh", neg_low, hidden_low, preferred_element_type=jnp.float32)
    slope_hid = (
        jnp.einsum("fh,bfwl->bhwl", out_weight, neg_low, preferred_element_type=jnp.float32)
        + slope_hidden
    )
    slope_mem = slope_hid * out_gate * (1.0 - squashed * squashed) + slope_memory
    gate_slope = jnp.concatenate(
        [
            slope_mem * update * in_gate * (1.0 - in_gate),
            slope_mem * memory * forget_gate * (1.0 - forget_gate),
            slope_hid * squashed * out_gate * (1.0 - out_gate),
            slope_mem * in_gate * (1.0 - update * update),
        ],
        axis=1,
    )
    grad_bias = jnp.sum(gate_slope, axis=(0, 2, 3))
    gate_low = gate_slope.astype(jnp.bfloat16)
    grad_lstm = kernel_slope(gate_low, joined_rim, "io")
    back_kernel = lstm_weight[::-1]
    if leading:
        back_kernel = back_kernel[:, :frames]
    gate_rimmed = padded_2(gate_low, (("band", 2),), 1)
    joined_slope = conv_three(back_kernel, gate_rimmed)
    cost_part = joined_slope[:, :frames]
    hidden_back = None if leading else joined_slope[:, frames:]
    slope_prev = slope_state + (obs_weight + prior_weight) * cost_part
    prior_low = (-prior_weight * cost_part).astype(jnp.bfloat16)
    grad_pout = kernel_slope(prior_low, latent_rim)
    latent_slope = conv_three(flipped(prior_out), rimmed_slope(prior_low))
    sigma = jax.nn.sigmoid(pre_prior)
    pre_low = (latent_slope * (sigma + pre_prior * sigma * (1.0 - sigma))).astype(jnp.bfloat16)
    grad_pin = kernel_slope(pre_low, state_rim)
    slope_prev = slope_prev + conv_three(flipped(prior_in), rimmed_slope(pre_low))
    memory_back = slope_mem * forget_gate
    return (
        slope_prev,
        hidden_back,
        memory_back,
        (grad_pin, grad_pout, grad_lstm, grad_bias, grad_outw),
    )


def body(
    first_guess,
    observed_height,
    swath_cells,
    drift_value,
    drift_cell,
    prior_in,
    prior_out,
    lstm_weight,
    lstm_bias,
    out_weight,
    final_slope,
):
    batch, frames, breadth, lat_count = first_guess.shape
    block = breadth * lat_count
    window_ids = jnp.arange(batch, dtype=jnp.int32)
    frame_ids = jnp.arange(frames, dtype=jnp.int32)
    placed = (
        window_ids[:, None, None, None] * frames + frame_ids[None, :, None, None]
    ) * block + swath_cells
    mask = (
        jnp.zeros((batch * frames * block,), jnp.float32)
        .at[placed.reshape(-1)]
        .set(1.0)
        .reshape(batch, frames, breadth, lat_count)
    )
    arrived = (
        lax.all_to_all(drift_value, "band", split_axis=2, concat_axis=1, tiled=True),
        lax.all_to_all(
            drift_cell.astype(jnp.float32), "band", split_axis=2, concat_axis=1, tiled=True
        ),
    )
    arrived_value = arrived[0]
    arrived_cell = arrived[1].astype(jnp.int32)
    occupied = arrived_cell >= 0
    target_idx = window_ids[:, None, None, None] * frames * block + jnp.where(
        occupied, arrived_cell, 0
    )
    drift_count = (
        jnp.zeros((batch * frames * block,), jnp.float32)
        .at[target_idx.reshape(-1)]
        .add(jnp.where(occupied, 1.0, 0.0).astype(jnp.float32).reshape(-1))
        .reshape(batch, frames, breadth, lat_count)
    )
    drift_total = (
        jnp.zeros((batch * frames * block,), jnp.float32)
        .at[target_idx.reshape(-1)]
        .add(jnp.where(occupied, arrived_value, 0.0).reshape(-1))
        .reshape(batch, frames, breadth, lat_count)
    )
    obs_weight = mask + drift_count
    obs_target = mask * observed_height + drift_total
    weights = (prior_in, prior_out, lstm_weight, lstm_bias, out_weight)
    units = out_weight.shape[1]
    blank = jnp.zeros((batch, units, breadth, lat_count), jnp.float32)
    state_one, hid_one, mem_one, saved_one = forward(
        first_guess, blank, blank, obs_weight, obs_target, weights
    )
    state_two, hid_two, mem_two, saved_two = forward(
        state_one, hid_one, mem_one, obs_weight, obs_target, weights
    )
    slope_mid, hidden_back, memory_back, grads_two = backward(
        final_slope, blank, blank, saved_two, obs_weight, weights, False
    )
    slope_start, unused_hid, unused_mem, grads_one = backward(
        slope_mid, hidden_back, memory_back, saved_one, obs_weight, weights, True
    )
    summed = jax.tree.map(jnp.add, grads_one, grads_two)
    cells_all = batch * lax.axis_size("win") * breadth * lax.axis_size("band") * lat_count
    scale = 1.0 / jnp.sqrt(jnp.float32(cells_all))
    flat = jnp.concatenate([member.reshape(-1) for member in summed])
    whole = summed_everywhere(flat, "band", "win")
    totals = []
    offset = 0
    for member in summed:
        length = member.size
        totals.append(whole[offset : offset + length].reshape(member.shape))
        offset = offset + length
    return (
        slope_start,
        totals[0] * scale,
        totals[1] * scale,
        totals[2] * scale,
        totals[3] * scale,
        totals[4] * scale,
    )


def summed_everywhere(flat, outer, inner):
    bands, wins = lax.axis_size(outer), lax.axis_size(inner)
    count = bands * wins
    if count & (count - 1):
        return lax.psum(flat, (outer, inner))
    axes = (outer, inner)
    inner_bits = wins.bit_length() - 1
    levels = (count.bit_length() - 1)
    order = ([inner_bits] if inner_bits < levels else []) + list(range(inner_bits)) + list(range(inner_bits + 1, levels))
    me = lax.axis_index(axes)
    extent = flat.shape[0]
    cur = jnp.pad(flat, (0, (-extent) % count))
    for level in order:
        mask = 1 << level
        half = cur.shape[0] // 2
        high = (me & mask) != 0
        low_part, high_part = cur[:half], cur[half:]
        keep = jnp.where(high, high_part, low_part)
        send = jnp.where(high, low_part, high_part)
        cur = keep + lax.ppermute(send, axes, [(i, i ^ mask) for i in range(count)])
    for level in reversed(order):
        mask = 1 << level
        high = (me & mask) != 0
        other = lax.ppermute(cur, axes, [(i, i ^ mask) for i in range(count)])
        cur = jnp.where(high, jnp.concatenate([other, cur]), jnp.concatenate([cur, other]))
    return cur[:extent]


def solution(mesh):
    return jax.shard_map(
        body,
        mesh=mesh,
        in_specs=(
            P("win", None, "band", None),
            P("win", None, "band", None),
            P("win", None, "band", None),
            P("win", "band", None, None),
            P("win", "band", None, None),
            P(),
            P(),
            P(),
            P(),
            P(),
            P("win", None, "band", None),
        ),
        out_specs=(P("win", None, "band", None), P(), P(), P(), P(), P()),
        check_vma=False,
    )
```

```python
import jax
import jax.numpy as jnp
from jax import lax
from jax.sharding import PartitionSpec as P

prior_weight = 1.0


def padded_2(array, sides, width):
    for axis, dim in sides:
        size, length = (lax.axis_size(axis), array.shape[dim])
        up = [(i, (i + 1) % size) for i in range(size - 1)]
        down = [(j, i) for i, j in up]
        last = lax.slice_in_dim(array, length - width, length, axis=dim)
        first = lax.slice_in_dim(array, 0, width, axis=dim)
        before = lax.ppermute(last, axis, up)
        after = lax.ppermute(first, axis, down)
        array = jnp.concatenate([before, array, after], axis=dim)
    return array


def conv_three(kernel, padded, form="oi"):
    breadth = padded.shape[2] - 2
    lat_count = padded.shape[3]
    framed = jnp.pad(padded, ((0, 0), (0, 0), (0, 0), (1, 1)))
    summed = None
    for lon_off in range(3):
        for lat_off in range(3):
            window = framed[:, :, lon_off : lon_off + breadth, lat_off : lat_off + lat_count]
            contrib = jnp.einsum(
                form + ",biwl->bowl",
                kernel[3 * lon_off + lat_off],
                window,
                preferred_element_type=jnp.float32,
            )
            summed = contrib if summed is None else summed + contrib
    return summed


def kernel_slope(cotangent, padded, form="oi"):
    breadth = cotangent.shape[2]
    lat_count = cotangent.shape[3]
    framed = jnp.pad(padded, ((0, 0), (0, 0), (0, 0), (1, 1)))
    pieces = []
    for lon_off in range(3):
        for lat_off in range(3):
            window = framed[:, :, lon_off : lon_off + breadth, lat_off : lat_off + lat_count]
            pieces.append(
                jnp.einsum(
                    "bowl,biwl->" + form, cotangent, window, preferred_element_type=jnp.float32
                )
            )
    return jnp.stack(pieces)


def flipped(kernel):
    return jnp.transpose(kernel[::-1], (0, 2, 1))


def rimmed_field(field):
    return padded_2(field, (("band", 2),), 1)


def rimmed_slope(field):
    return padded_2(field, (("band", 2),), 1)


def forward(current, hidden, memory, obs_weight, obs_target, weights):
    prior_in, prior_out, lstm_weight, lstm_bias, out_weight = weights
    units = out_weight.shape[1]
    state_rim = rimmed_field(current.astype(jnp.bfloat16))
    pre_prior = conv_three(prior_in, state_rim)
    latent = jax.nn.silu(pre_prior).astype(jnp.bfloat16)
    latent_rim = rimmed_field(latent)
    prior_state = conv_three(prior_out, latent_rim)
    cost_slope = obs_weight * current - obs_target + prior_weight * (current - prior_state)
    joined = jnp.concatenate([cost_slope, hidden], axis=1).astype(jnp.bfloat16)
    joined_rim = rimmed_field(joined)
    gate_all = conv_three(lstm_weight, joined_rim, "io") + lstm_bias[None, :, None, None]
    in_gate = jax.nn.sigmoid(gate_all[:, :units])
    forget_gate = jax.nn.sigmoid(gate_all[:, units : 2 * units])
    out_gate = jax.nn.sigmoid(gate_all[:, 2 * units : 3 * units])
    update = jnp.tanh(gate_all[:, 3 * units :])
    memory_next = forget_gate * memory + in_gate * update
    squashed = jnp.tanh(memory_next)
    hidden_next = out_gate * squashed
    hidden_low = hidden_next.astype(jnp.bfloat16)
    stepped = jnp.einsum(
        "fh,bhwl->bfwl", out_weight, hidden_low, preferred_element_type=jnp.float32
    )
    saved = (
        state_rim,
        pre_prior,
        latent_rim,
        joined_rim,
        in_gate,
        forget_gate,
        out_gate,
        update,
        memory,
        squashed,
        hidden_low,
    )
    return (current - stepped, hidden_next, memory_next, saved)


def backward(slope_state, slope_hidden, slope_memory, saved, obs_weight, weights, leading):
    prior_in, prior_out, lstm_weight, lstm_bias, out_weight = weights
    (
        state_rim,
        pre_prior,
        latent_rim,
        joined_rim,
        in_gate,
        forget_gate,
        out_gate,
        update,
        memory,
        squashed,
        hidden_low,
    ) = saved
    frames = slope_state.shape[1]
    neg_low = (-slope_state).astype(jnp.bfloat16)
    grad_outw = jnp.einsum("bfwl,bhwl->fh", neg_low, hidden_low, preferred_element_type=jnp.float32)
    slope_hid = (
        jnp.einsum("fh,bfwl->bhwl", out_weight, neg_low, preferred_element_type=jnp.float32)
        + slope_hidden
    )
    slope_mem = slope_hid * out_gate * (1.0 - squashed * squashed) + slope_memory
    gate_slope = jnp.concatenate(
        [
            slope_mem * update * in_gate * (1.0 - in_gate),
            slope_mem * memory * forget_gate * (1.0 - forget_gate),
            slope_hid * squashed * out_gate * (1.0 - out_gate),
            slope_mem * in_gate * (1.0 - update * update),
        ],
        axis=1,
    )
    grad_bias = jnp.sum(gate_slope, axis=(0, 2, 3))
    gate_low = gate_slope.astype(jnp.bfloat16)
    grad_lstm = kernel_slope(gate_low, joined_rim, "io")
    back_kernel = lstm_weight[::-1]
    if leading:
        back_kernel = back_kernel[:, :frames]
    gate_rimmed = padded_2(gate_low, (("band", 2),), 1)
    joined_slope = conv_three(back_kernel, gate_rimmed)
    cost_part = joined_slope[:, :frames]
    hidden_back = None if leading else joined_slope[:, frames:]
    slope_prev = slope_state + (obs_weight + prior_weight) * cost_part
    prior_low = (-prior_weight * cost_part).astype(jnp.bfloat16)
    grad_pout = kernel_slope(prior_low, latent_rim)
    latent_slope = conv_three(flipped(prior_out), rimmed_slope(prior_low))
    sigma = jax.nn.sigmoid(pre_prior)
    pre_low = (latent_slope * (sigma + pre_prior * sigma * (1.0 - sigma))).astype(jnp.bfloat16)
    grad_pin = kernel_slope(pre_low, state_rim)
    slope_prev = slope_prev + conv_three(flipped(prior_in), rimmed_slope(pre_low))
    memory_back = slope_mem * forget_gate
    return (
        slope_prev,
        hidden_back,
        memory_back,
        (grad_pin, grad_pout, grad_lstm, grad_bias, grad_outw),
    )


def body(
    first_guess,
    observed_height,
    swath_cells,
    drift_value,
    drift_cell,
    prior_in,
    prior_out,
    lstm_weight,
    lstm_bias,
    out_weight,
    final_slope,
):
    batch, frames, breadth, lat_count = first_guess.shape
    block = breadth * lat_count
    window_ids = jnp.arange(batch, dtype=jnp.int32)
    frame_ids = jnp.arange(frames, dtype=jnp.int32)
    placed = (
        window_ids[:, None, None, None] * frames + frame_ids[None, :, None, None]
    ) * block + swath_cells
    mask = (
        jnp.zeros((batch * frames * block,), jnp.float32)
        .at[placed.reshape(-1)]
        .set(1.0)
        .reshape(batch, frames, breadth, lat_count)
    )
    arrived = (
        lax.all_to_all(drift_value, "band", split_axis=2, concat_axis=1, tiled=True),
        lax.all_to_all(
            drift_cell.astype(jnp.float32), "band", split_axis=2, concat_axis=1, tiled=True
        ),
    )
    arrived_value = arrived[0]
    arrived_cell = arrived[1].astype(jnp.int32)
    occupied = arrived_cell >= 0
    target_idx = window_ids[:, None, None, None] * frames * block + jnp.where(
        occupied, arrived_cell, 0
    )
    drift_count = (
        jnp.zeros((batch * frames * block,), jnp.float32)
        .at[target_idx.reshape(-1)]
        .add(jnp.where(occupied, 1.0, 0.0).astype(jnp.float32).reshape(-1))
        .reshape(batch, frames, breadth, lat_count)
    )
    drift_total = (
        jnp.zeros((batch * frames * block,), jnp.float32)
        .at[target_idx.reshape(-1)]
        .add(jnp.where(occupied, arrived_value, 0.0).reshape(-1))
        .reshape(batch, frames, breadth, lat_count)
    )
    obs_weight = mask + drift_count
    obs_target = mask * observed_height + drift_total
    weights = (prior_in, prior_out, lstm_weight, lstm_bias, out_weight)
    units = out_weight.shape[1]
    blank = jnp.zeros((batch, units, breadth, lat_count), jnp.float32)
    state_one, hid_one, mem_one, saved_one = forward(
        first_guess, blank, blank, obs_weight, obs_target, weights
    )
    state_two, hid_two, mem_two, saved_two = forward(
        state_one, hid_one, mem_one, obs_weight, obs_target, weights
    )
    slope_mid, hidden_back, memory_back, grads_two = backward(
        final_slope, blank, blank, saved_two, obs_weight, weights, False
    )
    slope_start, unused_hid, unused_mem, grads_one = backward(
        slope_mid, hidden_back, memory_back, saved_one, obs_weight, weights, True
    )
    summed = jax.tree.map(jnp.add, grads_one, grads_two)
    cells_all = batch * lax.axis_size("win") * breadth * lax.axis_size("band") * lat_count
    scale = 1.0 / jnp.sqrt(jnp.float32(cells_all))
    grad_pin, grad_pout, grad_lstm, grad_bias, grad_outw = summed
    taps, ins, outs = grad_lstm.shape
    rows = jnp.pad(grad_lstm, ((0, 0), (0, (-ins) % 8), (0, 0))).reshape(-1, outs)
    lstm_total = summed_everywhere(rows, "band", "win")
    lstm_total = lstm_total.reshape(taps, -1, outs)[:, :ins]
    small = [grad_pin, grad_pout, grad_bias, grad_outw]
    flat = jnp.concatenate([member.reshape(-1) for member in small])
    flat = lax.psum(flat, ("band", "win"))
    totals = []
    offset = 0
    for member in small:
        length = member.size
        totals.append(flat[offset : offset + length].reshape(member.shape))
        offset = offset + length
    totals = [totals[0], totals[1], lstm_total, totals[2], totals[3]]
    return (
        slope_start,
        totals[0] * scale,
        totals[1] * scale,
        totals[2] * scale,
        totals[3] * scale,
        totals[4] * scale,
    )


def summed_everywhere(flat, outer, inner):
    bands, wins = lax.axis_size(outer), lax.axis_size(inner)
    count = bands * wins
    if count & (count - 1):
        return lax.psum(flat, (outer, inner))
    axes = (outer, inner)
    inner_bits = wins.bit_length() - 1
    levels = (count.bit_length() - 1)
    order = ([inner_bits] if inner_bits < levels else []) + list(range(inner_bits)) + list(range(inner_bits + 1, levels))
    me = lax.axis_index(axes)
    extent = flat.shape[0]
    cur = jnp.pad(flat, [(0, (-extent) % count)] + [(0, 0)] * (flat.ndim - 1))
    for level in order:
        mask = 1 << level
        half = cur.shape[0] // 2
        high = (me & mask) != 0
        low_part, high_part = cur[:half], cur[half:]
        keep = jnp.where(high, high_part, low_part)
        send = jnp.where(high, low_part, high_part)
        cur = keep + lax.ppermute(send, axes, [(i, i ^ mask) for i in range(count)])
    for level in reversed(order):
        mask = 1 << level
        high = (me & mask) != 0
        other = lax.ppermute(cur, axes, [(i, i ^ mask) for i in range(count)])
        cur = jnp.where(high, jnp.concatenate([other, cur]), jnp.concatenate([cur, other]))
    return cur[:extent]


def solution(mesh):
    return jax.shard_map(
        body,
        mesh=mesh,
        in_specs=(
            P("win", None, "band", None),
            P("win", None, "band", None),
            P("win", None, "band", None),
            P("win", "band", None, None),
            P("win", "band", None, None),
            P(),
            P(),
            P(),
            P(),
            P(),
            P("win", None, "band", None),
        ),
        out_specs=(P("win", None, "band", None), P(), P(), P(), P(), P()),
        check_vma=False,
    )
```

```python
import jax
import jax.numpy as jnp
from jax import lax
from jax.sharding import PartitionSpec as P

prior_weight = 1.0


def padded_2(array, sides, width):
    for axis, dim in sides:
        size, length = (lax.axis_size(axis), array.shape[dim])
        up = [(i, (i + 1) % size) for i in range(size - 1)]
        down = [(j, i) for i, j in up]
        last = lax.slice_in_dim(array, length - width, length, axis=dim)
        first = lax.slice_in_dim(array, 0, width, axis=dim)
        before = lax.ppermute(last, axis, up)
        after = lax.ppermute(first, axis, down)
        array = jnp.concatenate([before, array, after], axis=dim)
    return array


def conv_three(kernel, padded, form="oi"):
    breadth = padded.shape[2] - 2
    lat_count = padded.shape[3]
    framed = jnp.pad(padded, ((0, 0), (0, 0), (0, 0), (1, 1)))
    summed = None
    for lon_off in range(3):
        for lat_off in range(3):
            window = framed[:, :, lon_off : lon_off + breadth, lat_off : lat_off + lat_count]
            contrib = jnp.einsum(
                form + ",biwl->bowl",
                kernel[3 * lon_off + lat_off],
                window,
                preferred_element_type=jnp.float32,
            )
            summed = contrib if summed is None else summed + contrib
    return summed


def kernel_slope(cotangent, padded, form="oi"):
    breadth = cotangent.shape[2]
    lat_count = cotangent.shape[3]
    framed = jnp.pad(padded, ((0, 0), (0, 0), (0, 0), (1, 1)))
    pieces = []
    for lon_off in range(3):
        for lat_off in range(3):
            window = framed[:, :, lon_off : lon_off + breadth, lat_off : lat_off + lat_count]
            pieces.append(
                jnp.einsum(
                    "bowl,biwl->" + form, cotangent, window, preferred_element_type=jnp.float32
                )
            )
    return jnp.stack(pieces)


def flipped(kernel):
    return jnp.transpose(kernel[::-1], (0, 2, 1))


def rimmed_field(field):
    return padded_2(field, (("band", 2),), 1)


def rimmed_slope(field):
    return padded_2(field, (("band", 2),), 1)


def forward(current, hidden, memory, obs_weight, obs_target, weights):
    prior_in, prior_out, lstm_weight, lstm_bias, out_weight = weights
    units = out_weight.shape[1]
    state_rim = rimmed_field(current.astype(jnp.bfloat16))
    pre_prior = conv_three(prior_in, state_rim)
    latent = jax.nn.silu(pre_prior).astype(jnp.bfloat16)
    latent_rim = rimmed_field(latent)
    prior_state = conv_three(prior_out, latent_rim)
    cost_slope = obs_weight * current - obs_target + prior_weight * (current - prior_state)
    joined = jnp.concatenate([cost_slope, hidden], axis=1).astype(jnp.bfloat16)
    joined_rim = rimmed_field(joined)
    gate_all = conv_three(lstm_weight, joined_rim, "io") + lstm_bias[None, :, None, None]
    in_gate = jax.nn.sigmoid(gate_all[:, :units])
    forget_gate = jax.nn.sigmoid(gate_all[:, units : 2 * units])
    out_gate = jax.nn.sigmoid(gate_all[:, 2 * units : 3 * units])
    update = jnp.tanh(gate_all[:, 3 * units :])
    memory_next = forget_gate * memory + in_gate * update
    squashed = jnp.tanh(memory_next)
    hidden_next = out_gate * squashed
    hidden_low = hidden_next.astype(jnp.bfloat16)
    stepped = jnp.einsum(
        "fh,bhwl->bfwl", out_weight, hidden_low, preferred_element_type=jnp.float32
    )
    saved = (
        state_rim,
        pre_prior,
        latent_rim,
        joined_rim,
        in_gate,
        forget_gate,
        out_gate,
        update,
        memory,
        squashed,
        hidden_low,
    )
    return (current - stepped, hidden_next, memory_next, saved)


def backward(slope_state, slope_hidden, slope_memory, saved, obs_weight, weights, leading):
    prior_in, prior_out, lstm_weight, lstm_bias, out_weight = weights
    (
        state_rim,
        pre_prior,
        latent_rim,
        joined_rim,
        in_gate,
        forget_gate,
        out_gate,
        update,
        memory,
        squashed,
        hidden_low,
    ) = saved
    frames = slope_state.shape[1]
    neg_low = (-slope_state).astype(jnp.bfloat16)
    grad_outw = jnp.einsum("bfwl,bhwl->fh", neg_low, hidden_low, preferred_element_type=jnp.float32)
    slope_hid = (
        jnp.einsum("fh,bfwl->bhwl", out_weight, neg_low, preferred_element_type=jnp.float32)
        + slope_hidden
    )
    slope_mem = slope_hid * out_gate * (1.0 - squashed * squashed) + slope_memory
    gate_slope = jnp.concatenate(
        [
            slope_mem * update * in_gate * (1.0 - in_gate),
            slope_mem * memory * forget_gate * (1.0 - forget_gate),
            slope_hid * squashed * out_gate * (1.0 - out_gate),
            slope_mem * in_gate * (1.0 - update * update),
        ],
        axis=1,
    )
    grad_bias = jnp.sum(gate_slope, axis=(0, 2, 3))
    gate_low = gate_slope.astype(jnp.bfloat16)
    grad_lstm = kernel_slope(gate_low, joined_rim, "io")
    back_kernel = lstm_weight[::-1]
    if leading:
        back_kernel = back_kernel[:, :frames]
    gate_rimmed = padded_2(gate_low, (("band", 2),), 1)
    joined_slope = conv_three(back_kernel, gate_rimmed)
    cost_part = joined_slope[:, :frames]
    hidden_back = None if leading else joined_slope[:, frames:]
    slope_prev = slope_state + (obs_weight + prior_weight) * cost_part
    prior_low = (-prior_weight * cost_part).astype(jnp.bfloat16)
    grad_pout = kernel_slope(prior_low, latent_rim)
    latent_slope = conv_three(flipped(prior_out), rimmed_slope(prior_low))
    sigma = jax.nn.sigmoid(pre_prior)
    pre_low = (latent_slope * (sigma + pre_prior * sigma * (1.0 - sigma))).astype(jnp.bfloat16)
    grad_pin = kernel_slope(pre_low, state_rim)
    slope_prev = slope_prev + conv_three(flipped(prior_in), rimmed_slope(pre_low))
    memory_back = slope_mem * forget_gate
    return (
        slope_prev,
        hidden_back,
        memory_back,
        (grad_pin, grad_pout, grad_lstm, grad_bias, grad_outw),
    )


def body(
    first_guess,
    observed_height,
    swath_cells,
    drift_value,
    drift_cell,
    prior_in,
    prior_out,
    lstm_weight,
    lstm_bias,
    out_weight,
    final_slope,
):
    batch, frames, breadth, lat_count = first_guess.shape
    block = breadth * lat_count
    window_ids = jnp.arange(batch, dtype=jnp.int32)
    frame_ids = jnp.arange(frames, dtype=jnp.int32)
    placed = (
        window_ids[:, None, None, None] * frames + frame_ids[None, :, None, None]
    ) * block + swath_cells
    mask = (
        jnp.zeros((batch * frames * block,), jnp.float32)
        .at[placed.reshape(-1)]
        .set(1.0)
        .reshape(batch, frames, breadth, lat_count)
    )
    arrived = (
        lax.all_to_all(drift_value, "band", split_axis=2, concat_axis=1, tiled=True),
        lax.all_to_all(
            drift_cell.astype(jnp.float32), "band", split_axis=2, concat_axis=1, tiled=True
        ),
    )
    arrived_value = arrived[0]
    arrived_cell = arrived[1].astype(jnp.int32)
    occupied = arrived_cell >= 0
    target_idx = window_ids[:, None, None, None] * frames * block + jnp.where(
        occupied, arrived_cell, 0
    )
    drift_count = (
        jnp.zeros((batch * frames * block,), jnp.float32)
        .at[target_idx.reshape(-1)]
        .add(jnp.where(occupied, 1.0, 0.0).astype(jnp.float32).reshape(-1))
        .reshape(batch, frames, breadth, lat_count)
    )
    drift_total = (
        jnp.zeros((batch * frames * block,), jnp.float32)
        .at[target_idx.reshape(-1)]
        .add(jnp.where(occupied, arrived_value, 0.0).reshape(-1))
        .reshape(batch, frames, breadth, lat_count)
    )
    obs_weight = mask + drift_count
    obs_target = mask * observed_height + drift_total
    weights = (prior_in, prior_out, lstm_weight, lstm_bias, out_weight)
    units = out_weight.shape[1]
    blank = jnp.zeros((batch, units, breadth, lat_count), jnp.float32)
    state_one, hid_one, mem_one, saved_one = forward(
        first_guess, blank, blank, obs_weight, obs_target, weights
    )
    state_two, hid_two, mem_two, saved_two = forward(
        state_one, hid_one, mem_one, obs_weight, obs_target, weights
    )
    slope_mid, hidden_back, memory_back, grads_two = backward(
        final_slope, blank, blank, saved_two, obs_weight, weights, False
    )
    slope_start, unused_hid, unused_mem, grads_one = backward(
        slope_mid, hidden_back, memory_back, saved_one, obs_weight, weights, True
    )
    summed = jax.tree.map(jnp.add, grads_one, grads_two)
    cells_all = batch * lax.axis_size("win") * breadth * lax.axis_size("band") * lat_count
    scale = 1.0 / jnp.sqrt(jnp.float32(cells_all))
    grad_pin, grad_pout, grad_lstm, grad_bias, grad_outw = summed
    taps, ins, outs = grad_lstm.shape
    rows = jnp.pad(grad_lstm, ((0, 0), (0, (-ins) % 8), (0, 0))).reshape(-1, outs)
    lstm_total = summed_everywhere(rows, "band", "win")
    lstm_total = lstm_total.reshape(taps, -1, outs)[:, :ins]
    small = [grad_pin, grad_pout, grad_bias, grad_outw]
    flat = jnp.concatenate([member.reshape(-1) for member in small])
    flat = summed_everywhere(flat, "band", "win")
    totals = []
    offset = 0
    for member in small:
        length = member.size
        totals.append(flat[offset : offset + length].reshape(member.shape))
        offset = offset + length
    totals = [totals[0], totals[1], lstm_total, totals[2], totals[3]]
    return (
        slope_start,
        totals[0] * scale,
        totals[1] * scale,
        totals[2] * scale,
        totals[3] * scale,
        totals[4] * scale,
    )


def summed_everywhere(flat, outer, inner):
    bands, wins = lax.axis_size(outer), lax.axis_size(inner)
    count = bands * wins
    if count & (count - 1):
        return lax.psum(flat, (outer, inner))
    axes = (outer, inner)
    inner_bits = wins.bit_length() - 1
    levels = (count.bit_length() - 1)
    order = ([inner_bits] if inner_bits < levels else []) + list(range(inner_bits)) + list(range(inner_bits + 1, levels))
    me = lax.axis_index(axes)
    extent = flat.shape[0]
    cur = jnp.pad(flat, [(0, (-extent) % count)] + [(0, 0)] * (flat.ndim - 1))
    for level in order:
        mask = 1 << level
        half = cur.shape[0] // 2
        high = (me & mask) != 0
        low_part, high_part = cur[:half], cur[half:]
        keep = jnp.where(high, high_part, low_part)
        send = jnp.where(high, low_part, high_part)
        cur = keep + lax.ppermute(send, axes, [(i, i ^ mask) for i in range(count)])
    for level in reversed(order):
        mask = 1 << level
        high = (me & mask) != 0
        other = lax.ppermute(cur, axes, [(i, i ^ mask) for i in range(count)])
        cur = jnp.where(high, jnp.concatenate([other, cur]), jnp.concatenate([cur, other]))
    return cur[:extent]


def solution(mesh):
    return jax.shard_map(
        body,
        mesh=mesh,
        in_specs=(
            P("win", None, "band", None),
            P("win", None, "band", None),
            P("win", None, "band", None),
            P("win", "band", None, None),
            P("win", "band", None, None),
            P(),
            P(),
            P(),
            P(),
            P(),
            P("win", None, "band", None),
        ),
        out_specs=(P("win", None, "band", None), P(), P(), P(), P(), P()),
        check_vma=False,
    )
```

```python
import jax
import jax.numpy as jnp
from jax import lax
from jax.sharding import PartitionSpec as P

prior_weight = 1.0


def padded_2(array, sides, width):
    for axis, dim in sides:
        size, length = (lax.axis_size(axis), array.shape[dim])
        up = [(i, (i + 1) % size) for i in range(size - 1)]
        down = [(j, i) for i, j in up]
        last = lax.slice_in_dim(array, length - width, length, axis=dim)
        first = lax.slice_in_dim(array, 0, width, axis=dim)
        before = lax.ppermute(last, axis, up)
        after = lax.ppermute(first, axis, down)
        array = jnp.concatenate([before, array, after], axis=dim)
    return array


def conv_three(kernel, padded, form="oi"):
    taps, first, second = kernel.shape
    spread = kernel.reshape(3, 3, first, second)
    dims = ("HWOI", "HWIO")[form == "io"]
    return lax.conv_general_dilated(
        padded,
        spread,
        window_strides=(1, 1),
        padding=((0, 0), (1, 1)),
        dimension_numbers=("NCHW", dims, "NCHW"),
        preferred_element_type=jnp.float32,
    )


def kernel_slope(cotangent, padded, form="oi"):
    outs = cotangent.shape[1]
    ins = padded.shape[1]
    picked = (3, 2, 0, 1) if form == "oi" else (2, 3, 0, 1)
    numbers = lax.ConvDimensionNumbers(lhs_spec=(1, 0, 2, 3), rhs_spec=(1, 0, 2, 3), out_spec=picked)
    slope = lax.conv_general_dilated(
        padded,
        cotangent,
        window_strides=(1, 1),
        padding=((0, 0), (1, 1)),
        dimension_numbers=numbers,
        preferred_element_type=jnp.float32,
    )
    return slope.reshape((9,) + slope.shape[2:])


def flipped(kernel):
    return jnp.transpose(kernel[::-1], (0, 2, 1))


def rimmed_field(field):
    return padded_2(field, (("band", 2),), 1)


def rimmed_slope(field):
    return padded_2(field, (("band", 2),), 1)


def forward(current, hidden, memory, obs_weight, obs_target, weights):
    prior_in, prior_out, lstm_weight, lstm_bias, out_weight = weights
    units = out_weight.shape[1]
    state_rim = rimmed_field(current.astype(jnp.bfloat16))
    pre_prior = conv_three(prior_in, state_rim)
    latent = jax.nn.silu(pre_prior).astype(jnp.bfloat16)
    latent_rim = rimmed_field(latent)
    prior_state = conv_three(prior_out, latent_rim)
    cost_slope = obs_weight * current - obs_target + prior_weight * (current - prior_state)
    joined = jnp.concatenate([cost_slope, hidden], axis=1).astype(jnp.bfloat16)
    joined_rim = rimmed_field(joined)
    gate_all = conv_three(lstm_weight, joined_rim, "io") + lstm_bias[None, :, None, None]
    in_gate = jax.nn.sigmoid(gate_all[:, :units])
    forget_gate = jax.nn.sigmoid(gate_all[:, units : 2 * units])
    out_gate = jax.nn.sigmoid(gate_all[:, 2 * units : 3 * units])
    update = jnp.tanh(gate_all[:, 3 * units :])
    memory_next = forget_gate * memory + in_gate * update
    squashed = jnp.tanh(memory_next)
    hidden_next = out_gate * squashed
    hidden_low = hidden_next.astype(jnp.bfloat16)
    stepped = jnp.einsum(
        "fh,bhwl->bfwl", out_weight, hidden_low, preferred_element_type=jnp.float32
    )
    saved = (
        state_rim,
        pre_prior,
        latent_rim,
        joined_rim,
        in_gate,
        forget_gate,
        out_gate,
        update,
        memory,
        squashed,
        hidden_low,
    )
    return (current - stepped, hidden_next, memory_next, saved)


def backward(slope_state, slope_hidden, slope_memory, saved, obs_weight, weights, leading):
    prior_in, prior_out, lstm_weight, lstm_bias, out_weight = weights
    (
        state_rim,
        pre_prior,
        latent_rim,
        joined_rim,
        in_gate,
        forget_gate,
        out_gate,
        update,
        memory,
        squashed,
        hidden_low,
    ) = saved
    frames = slope_state.shape[1]
    neg_low = (-slope_state).astype(jnp.bfloat16)
    grad_outw = jnp.einsum("bfwl,bhwl->fh", neg_low, hidden_low, preferred_element_type=jnp.float32)
    slope_hid = (
        jnp.einsum("fh,bfwl->bhwl", out_weight, neg_low, preferred_element_type=jnp.float32)
        + slope_hidden
    )
    slope_mem = slope_hid * out_gate * (1.0 - squashed * squashed) + slope_memory
    gate_slope = jnp.concatenate(
        [
            slope_mem * update * in_gate * (1.0 - in_gate),
            slope_mem * memory * forget_gate * (1.0 - forget_gate),
            slope_hid * squashed * out_gate * (1.0 - out_gate),
            slope_mem * in_gate * (1.0 - update * update),
        ],
        axis=1,
    )
    grad_bias = jnp.sum(gate_slope, axis=(0, 2, 3))
    gate_low = gate_slope.astype(jnp.bfloat16)
    grad_lstm = kernel_slope(gate_low, joined_rim, "io")
    back_kernel = lstm_weight[::-1]
    if leading:
        back_kernel = back_kernel[:, :frames]
    gate_rimmed = padded_2(gate_low, (("band", 2),), 1)
    joined_slope = conv_three(back_kernel, gate_rimmed)
    cost_part = joined_slope[:, :frames]
    hidden_back = None if leading else joined_slope[:, frames:]
    slope_prev = slope_state + (obs_weight + prior_weight) * cost_part
    prior_low = (-prior_weight * cost_part).astype(jnp.bfloat16)
    grad_pout = kernel_slope(prior_low, latent_rim)
    latent_slope = conv_three(flipped(prior_out), rimmed_slope(prior_low))
    sigma = jax.nn.sigmoid(pre_prior)
    pre_low = (latent_slope * (sigma + pre_prior * sigma * (1.0 - sigma))).astype(jnp.bfloat16)
    grad_pin = kernel_slope(pre_low, state_rim)
    slope_prev = slope_prev + conv_three(flipped(prior_in), rimmed_slope(pre_low))
    memory_back = slope_mem * forget_gate
    return (
        slope_prev,
        hidden_back,
        memory_back,
        (grad_pin, grad_pout, grad_lstm, grad_bias, grad_outw),
    )


def body(
    first_guess,
    observed_height,
    swath_cells,
    drift_value,
    drift_cell,
    prior_in,
    prior_out,
    lstm_weight,
    lstm_bias,
    out_weight,
    final_slope,
):
    batch, frames, breadth, lat_count = first_guess.shape
    block = breadth * lat_count
    window_ids = jnp.arange(batch, dtype=jnp.int32)
    frame_ids = jnp.arange(frames, dtype=jnp.int32)
    placed = (
        window_ids[:, None, None, None] * frames + frame_ids[None, :, None, None]
    ) * block + swath_cells
    mask = (
        jnp.zeros((batch * frames * block,), jnp.float32)
        .at[placed.reshape(-1)]
        .set(1.0)
        .reshape(batch, frames, breadth, lat_count)
    )
    arrived = (
        lax.all_to_all(drift_value, "band", split_axis=2, concat_axis=1, tiled=True),
        lax.all_to_all(
            drift_cell.astype(jnp.float32), "band", split_axis=2, concat_axis=1, tiled=True
        ),
    )
    arrived_value = arrived[0]
    arrived_cell = arrived[1].astype(jnp.int32)
    occupied = arrived_cell >= 0
    target_idx = window_ids[:, None, None, None] * frames * block + jnp.where(
        occupied, arrived_cell, 0
    )
    drift_count = (
        jnp.zeros((batch * frames * block,), jnp.float32)
        .at[target_idx.reshape(-1)]
        .add(jnp.where(occupied, 1.0, 0.0).astype(jnp.float32).reshape(-1))
        .reshape(batch, frames, breadth, lat_count)
    )
    drift_total = (
        jnp.zeros((batch * frames * block,), jnp.float32)
        .at[target_idx.reshape(-1)]
        .add(jnp.where(occupied, arrived_value, 0.0).reshape(-1))
        .reshape(batch, frames, breadth, lat_count)
    )
    obs_weight = mask + drift_count
    obs_target = mask * observed_height + drift_total
    weights = (prior_in, prior_out, lstm_weight, lstm_bias, out_weight)
    units = out_weight.shape[1]
    blank = jnp.zeros((batch, units, breadth, lat_count), jnp.float32)
    state_one, hid_one, mem_one, saved_one = forward(
        first_guess, blank, blank, obs_weight, obs_target, weights
    )
    state_two, hid_two, mem_two, saved_two = forward(
        state_one, hid_one, mem_one, obs_weight, obs_target, weights
    )
    slope_mid, hidden_back, memory_back, grads_two = backward(
        final_slope, blank, blank, saved_two, obs_weight, weights, False
    )
    slope_start, unused_hid, unused_mem, grads_one = backward(
        slope_mid, hidden_back, memory_back, saved_one, obs_weight, weights, True
    )
    summed = jax.tree.map(jnp.add, grads_one, grads_two)
    cells_all = batch * lax.axis_size("win") * breadth * lax.axis_size("band") * lat_count
    scale = 1.0 / jnp.sqrt(jnp.float32(cells_all))
    grad_pin, grad_pout, grad_lstm, grad_bias, grad_outw = summed
    taps, ins, outs = grad_lstm.shape
    rows = jnp.pad(grad_lstm, ((0, 0), (0, (-ins) % 8), (0, 0))).reshape(-1, outs)
    lstm_total = summed_everywhere(rows, "band", "win")
    lstm_total = lstm_total.reshape(taps, -1, outs)[:, :ins]
    small = [grad_pin, grad_pout, grad_bias, grad_outw]
    flat = jnp.concatenate([member.reshape(-1) for member in small])
    flat = summed_everywhere(flat, "band", "win")
    totals = []
    offset = 0
    for member in small:
        length = member.size
        totals.append(flat[offset : offset + length].reshape(member.shape))
        offset = offset + length
    totals = [totals[0], totals[1], lstm_total, totals[2], totals[3]]
    return (
        slope_start,
        totals[0] * scale,
        totals[1] * scale,
        totals[2] * scale,
        totals[3] * scale,
        totals[4] * scale,
    )


def summed_everywhere(flat, outer, inner):
    bands, wins = lax.axis_size(outer), lax.axis_size(inner)
    count = bands * wins
    if count & (count - 1):
        return lax.psum(flat, (outer, inner))
    axes = (outer, inner)
    inner_bits = wins.bit_length() - 1
    levels = (count.bit_length() - 1)
    order = ([inner_bits] if inner_bits < levels else []) + list(range(inner_bits)) + list(range(inner_bits + 1, levels))
    me = lax.axis_index(axes)
    extent = flat.shape[0]
    cur = jnp.pad(flat, [(0, (-extent) % count)] + [(0, 0)] * (flat.ndim - 1))
    for level in order:
        mask = 1 << level
        half = cur.shape[0] // 2
        high = (me & mask) != 0
        low_part, high_part = cur[:half], cur[half:]
        keep = jnp.where(high, high_part, low_part)
        send = jnp.where(high, low_part, high_part)
        cur = keep + lax.ppermute(send, axes, [(i, i ^ mask) for i in range(count)])
    for level in reversed(order):
        mask = 1 << level
        high = (me & mask) != 0
        other = lax.ppermute(cur, axes, [(i, i ^ mask) for i in range(count)])
        cur = jnp.where(high, jnp.concatenate([other, cur]), jnp.concatenate([cur, other]))
    return cur[:extent]


def solution(mesh):
    return jax.shard_map(
        body,
        mesh=mesh,
        in_specs=(
            P("win", None, "band", None),
            P("win", None, "band", None),
            P("win", None, "band", None),
            P("win", "band", None, None),
            P("win", "band", None, None),
            P(),
            P(),
            P(),
            P(),
            P(),
            P("win", None, "band", None),
        ),
        out_specs=(P("win", None, "band", None), P(), P(), P(), P(), P()),
        check_vma=False,
    )
```

```python
import jax
import jax.numpy as jnp
from jax import lax
from jax.sharding import PartitionSpec as P

prior_weight = 1.0


def padded_2(array, sides, width):
    for axis, dim in sides:
        size, length = (lax.axis_size(axis), array.shape[dim])
        up = [(i, (i + 1) % size) for i in range(size - 1)]
        down = [(j, i) for i, j in up]
        last = lax.slice_in_dim(array, length - width, length, axis=dim)
        first = lax.slice_in_dim(array, 0, width, axis=dim)
        before = lax.ppermute(last, axis, up)
        after = lax.ppermute(first, axis, down)
        array = jnp.concatenate([before, array, after], axis=dim)
    return array


def conv_three(kernel, padded, form="oi"):
    breadth = padded.shape[2] - 2
    lat_count = padded.shape[3]
    framed = jnp.pad(padded, ((0, 0), (0, 0), (0, 0), (1, 1)))
    summed = None
    for lon_off in range(3):
        for lat_off in range(3):
            window = framed[:, :, lon_off : lon_off + breadth, lat_off : lat_off + lat_count]
            contrib = jnp.einsum(
                form + ",biwl->bowl",
                kernel[3 * lon_off + lat_off],
                window,
                preferred_element_type=jnp.float32,
            )
            summed = contrib if summed is None else summed + contrib
    return summed


def kernel_slope(cotangent, padded, form="oi"):
    breadth = cotangent.shape[2]
    lat_count = cotangent.shape[3]
    framed = jnp.pad(padded, ((0, 0), (0, 0), (0, 0), (1, 1)))
    pieces = []
    for lon_off in range(3):
        for lat_off in range(3):
            window = framed[:, :, lon_off : lon_off + breadth, lat_off : lat_off + lat_count]
            pieces.append(
                jnp.einsum(
                    "bowl,biwl->" + form, cotangent, window, preferred_element_type=jnp.float32
                )
            )
    return jnp.stack(pieces)


def flipped(kernel):
    return jnp.transpose(kernel[::-1], (0, 2, 1))


def rimmed_field(field):
    return padded_2(field, (("band", 2),), 1)


def rimmed_slope(field):
    return padded_2(field, (("band", 2),), 1)


def forward(current, hidden, memory, obs_weight, obs_target, weights):
    prior_in, prior_out, lstm_weight, lstm_bias, out_weight = weights
    units = out_weight.shape[1]
    state_rim = rimmed_field(current.astype(jnp.bfloat16))
    pre_prior = conv_three(prior_in, state_rim)
    latent = jax.nn.silu(pre_prior).astype(jnp.bfloat16)
    latent_rim = rimmed_field(latent)
    prior_state = conv_three(prior_out, latent_rim)
    cost_slope = obs_weight * current - obs_target + prior_weight * (current - prior_state)
    joined = jnp.concatenate([cost_slope, hidden], axis=1).astype(jnp.bfloat16)
    joined_rim = rimmed_field(joined)
    gate_all = conv_three(lstm_weight, joined_rim, "io") + lstm_bias[None, :, None, None]
    in_gate = jax.nn.sigmoid(gate_all[:, :units])
    forget_gate = jax.nn.sigmoid(gate_all[:, units : 2 * units])
    out_gate = jax.nn.sigmoid(gate_all[:, 2 * units : 3 * units])
    update = jnp.tanh(gate_all[:, 3 * units :])
    memory_next = forget_gate * memory + in_gate * update
    squashed = jnp.tanh(memory_next)
    hidden_next = out_gate * squashed
    hidden_low = hidden_next.astype(jnp.bfloat16)
    stepped = jnp.einsum(
        "fh,bhwl->bfwl", out_weight, hidden_low, preferred_element_type=jnp.float32
    )
    saved = (
        state_rim,
        pre_prior,
        latent_rim,
        joined_rim,
        in_gate,
        forget_gate,
        out_gate,
        update,
        memory,
        squashed,
        hidden_low,
    )
    return (current - stepped, hidden_next, memory_next, saved)


def backward(slope_state, slope_hidden, slope_memory, saved, obs_weight, weights, leading):
    prior_in, prior_out, lstm_weight, lstm_bias, out_weight = weights
    (
        state_rim,
        pre_prior,
        latent_rim,
        joined_rim,
        in_gate,
        forget_gate,
        out_gate,
        update,
        memory,
        squashed,
        hidden_low,
    ) = saved
    frames = slope_state.shape[1]
    neg_low = (-slope_state).astype(jnp.bfloat16)
    grad_outw = jnp.einsum("bfwl,bhwl->fh", neg_low, hidden_low, preferred_element_type=jnp.float32)
    slope_hid = (
        jnp.einsum("fh,bfwl->bhwl", out_weight, neg_low, preferred_element_type=jnp.float32)
        + slope_hidden
    )
    slope_mem = slope_hid * out_gate * (1.0 - squashed * squashed) + slope_memory
    gate_slope = jnp.concatenate(
        [
            slope_mem * update * in_gate * (1.0 - in_gate),
            slope_mem * memory * forget_gate * (1.0 - forget_gate),
            slope_hid * squashed * out_gate * (1.0 - out_gate),
            slope_mem * in_gate * (1.0 - update * update),
        ],
        axis=1,
    )
    grad_bias = jnp.sum(gate_slope, axis=(0, 2, 3))
    gate_low = gate_slope.astype(jnp.bfloat16)
    grad_lstm = kernel_slope(gate_low, joined_rim, "io")
    back_kernel = lstm_weight[::-1]
    if leading:
        back_kernel = back_kernel[:, :frames]
    gate_rimmed = padded_2(gate_low, (("band", 2),), 1)
    joined_slope = conv_three(back_kernel, gate_rimmed)
    cost_part = joined_slope[:, :frames]
    hidden_back = None if leading else joined_slope[:, frames:]
    slope_prev = slope_state + (obs_weight + prior_weight) * cost_part
    prior_low = (-prior_weight * cost_part).astype(jnp.bfloat16)
    grad_pout = kernel_slope(prior_low, latent_rim)
    latent_slope = conv_three(flipped(prior_out), rimmed_slope(prior_low))
    sigma = jax.nn.sigmoid(pre_prior)
    pre_low = (latent_slope * (sigma + pre_prior * sigma * (1.0 - sigma))).astype(jnp.bfloat16)
    grad_pin = kernel_slope(pre_low, state_rim)
    slope_prev = slope_prev + conv_three(flipped(prior_in), rimmed_slope(pre_low))
    memory_back = slope_mem * forget_gate
    return (
        slope_prev,
        hidden_back,
        memory_back,
        (grad_pin, grad_pout, grad_lstm, grad_bias, grad_outw),
    )


def body(
    first_guess,
    observed_height,
    swath_cells,
    drift_value,
    drift_cell,
    prior_in,
    prior_out,
    lstm_weight,
    lstm_bias,
    out_weight,
    final_slope,
):
    batch, frames, breadth, lat_count = first_guess.shape
    block = breadth * lat_count
    spots = jnp.arange(block, dtype=jnp.int32)
    hits = swath_cells[:, :, 0, :, None] == spots
    mask = jnp.any(hits, axis=2).astype(jnp.float32).reshape(batch, frames, breadth, lat_count)
    packed = jnp.stack([drift_value, drift_cell.astype(jnp.float32)])
    arrived = lax.all_to_all(packed, "band", split_axis=3, concat_axis=2, tiled=True)
    arrived_value = arrived[0].reshape(batch, -1)
    arrived_cell = arrived[1].astype(jnp.int32).reshape(batch, -1)
    places = jnp.arange(frames * block, dtype=jnp.int32).reshape(frames, breadth, lat_count)
    landed = arrived_cell[:, :, None, None, None] == places
    drift_count = jnp.sum(landed.astype(jnp.float32), axis=1)
    drift_total = jnp.sum(jnp.where(landed, arrived_value[:, :, None, None, None], 0.0), axis=1)
    obs_weight = mask + drift_count
    obs_target = mask * observed_height + drift_total
    weights = (prior_in, prior_out, lstm_weight, lstm_bias, out_weight)
    units = out_weight.shape[1]
    blank = jnp.zeros((batch, units, breadth, lat_count), jnp.float32)
    state_one, hid_one, mem_one, saved_one = forward(
        first_guess, blank, blank, obs_weight, obs_target, weights
    )
    state_two, hid_two, mem_two, saved_two = forward(
        state_one, hid_one, mem_one, obs_weight, obs_target, weights
    )
    slope_mid, hidden_back, memory_back, grads_two = backward(
        final_slope, blank, blank, saved_two, obs_weight, weights, False
    )
    slope_start, unused_hid, unused_mem, grads_one = backward(
        slope_mid, hidden_back, memory_back, saved_one, obs_weight, weights, True
    )
    summed = jax.tree.map(jnp.add, grads_one, grads_two)
    cells_all = batch * lax.axis_size("win") * breadth * lax.axis_size("band") * lat_count
    scale = 1.0 / jnp.sqrt(jnp.float32(cells_all))
    grad_pin, grad_pout, grad_lstm, grad_bias, grad_outw = summed
    taps, ins, outs = grad_lstm.shape
    rows = jnp.pad(grad_lstm, ((0, 0), (0, (-ins) % 8), (0, 0))).reshape(-1, outs)
    lstm_total = summed_everywhere(rows, "band", "win")
    lstm_total = lstm_total.reshape(taps, -1, outs)[:, :ins]
    small = [grad_pin, grad_pout, grad_bias, grad_outw]
    flat = jnp.concatenate([member.reshape(-1) for member in small])
    flat = summed_everywhere(flat, "band", "win")
    totals = []
    offset = 0
    for member in small:
        length = member.size
        totals.append(flat[offset : offset + length].reshape(member.shape))
        offset = offset + length
    totals = [totals[0], totals[1], lstm_total, totals[2], totals[3]]
    return (
        slope_start,
        totals[0] * scale,
        totals[1] * scale,
        totals[2] * scale,
        totals[3] * scale,
        totals[4] * scale,
    )


def summed_everywhere(flat, outer, inner):
    bands, wins = lax.axis_size(outer), lax.axis_size(inner)
    count = bands * wins
    if count & (count - 1):
        return lax.psum(flat, (outer, inner))
    axes = (outer, inner)
    inner_bits = wins.bit_length() - 1
    levels = (count.bit_length() - 1)
    order = ([inner_bits] if inner_bits < levels else []) + list(range(inner_bits)) + list(range(inner_bits + 1, levels))
    me = lax.axis_index(axes)
    extent = flat.shape[0]
    cur = jnp.pad(flat, [(0, (-extent) % count)] + [(0, 0)] * (flat.ndim - 1))
    for level in order:
        mask = 1 << level
        half = cur.shape[0] // 2
        high = (me & mask) != 0
        low_part, high_part = cur[:half], cur[half:]
        keep = jnp.where(high, high_part, low_part)
        send = jnp.where(high, low_part, high_part)
        cur = keep + lax.ppermute(send, axes, [(i, i ^ mask) for i in range(count)])
    for level in reversed(order):
        mask = 1 << level
        high = (me & mask) != 0
        other = lax.ppermute(cur, axes, [(i, i ^ mask) for i in range(count)])
        cur = jnp.where(high, jnp.concatenate([other, cur]), jnp.concatenate([cur, other]))
    return cur[:extent]


def solution(mesh):
    return jax.shard_map(
        body,
        mesh=mesh,
        in_specs=(
            P("win", None, "band", None),
            P("win", None, "band", None),
            P("win", None, "band", None),
            P("win", "band", None, None),
            P("win", "band", None, None),
            P(),
            P(),
            P(),
            P(),
            P(),
            P("win", None, "band", None),
        ),
        out_specs=(P("win", None, "band", None), P(), P(), P(), P(), P()),
        check_vma=False,
    )
```

```python
import jax
import jax.numpy as jnp
from jax import lax
from jax.sharding import PartitionSpec as P

prior_weight = 1.0


def padded_2(array, sides, width):
    for axis, dim in sides:
        size, length = (lax.axis_size(axis), array.shape[dim])
        up = [(i, (i + 1) % size) for i in range(size - 1)]
        down = [(j, i) for i, j in up]
        last = lax.slice_in_dim(array, length - width, length, axis=dim)
        first = lax.slice_in_dim(array, 0, width, axis=dim)
        before = lax.ppermute(last, axis, up)
        after = lax.ppermute(first, axis, down)
        array = jnp.concatenate([before, array, after], axis=dim)
    return array


def conv_three(kernel, padded, form="oi"):
    breadth = padded.shape[2] - 2
    lat_count = padded.shape[3]
    framed = jnp.pad(padded, ((0, 0), (0, 0), (0, 0), (1, 1)))
    summed = None
    for lon_off in range(3):
        for lat_off in range(3):
            window = framed[:, :, lon_off : lon_off + breadth, lat_off : lat_off + lat_count]
            contrib = jnp.einsum(
                form + ",biwl->bowl",
                kernel[3 * lon_off + lat_off],
                window,
                preferred_element_type=jnp.float32,
            )
            summed = contrib if summed is None else summed + contrib
    return summed


def kernel_slope(cotangent, padded, form="oi"):
    breadth = cotangent.shape[2]
    lat_count = cotangent.shape[3]
    framed = jnp.pad(padded, ((0, 0), (0, 0), (0, 0), (1, 1)))
    pieces = []
    for lon_off in range(3):
        for lat_off in range(3):
            window = framed[:, :, lon_off : lon_off + breadth, lat_off : lat_off + lat_count]
            pieces.append(
                jnp.einsum(
                    "bowl,biwl->" + form, cotangent, window, preferred_element_type=jnp.float32
                )
            )
    return jnp.stack(pieces)


def flipped(kernel):
    return jnp.transpose(kernel[::-1], (0, 2, 1))


def rimmed_field(field):
    return padded_2(field, (("band", 2),), 1)


def edge_zeroed(field):
    place = lax.axis_index("band")
    last = lax.axis_size("band") - 1
    width = field.shape[2]
    column = lax.broadcasted_iota(jnp.int32, (1, 1, width, 1), 2)
    outside = ((place == 0) & (column == 0)) | ((place == last) & (column == width - 1))
    return jnp.where(outside, jnp.zeros_like(field), field)


def rimmed_slope(field):
    return padded_2(field, (("band", 2),), 1)


def forward(current, hidden, memory, obs_weight, obs_target, weights):
    prior_in, prior_out, lstm_weight, lstm_bias, out_weight = weights
    units = out_weight.shape[1]
    state_wide = padded_2(current.astype(jnp.bfloat16), (("band", 2),), 2)
    state_rim = state_wide[:, :, 1:-1]
    pre_prior = conv_three(prior_in, state_wide)
    latent_rim = edge_zeroed(jax.nn.silu(pre_prior).astype(jnp.bfloat16))
    prior_state = conv_three(prior_out, latent_rim)
    cost_slope = obs_weight * current - obs_target + prior_weight * (current - prior_state)
    joined = jnp.concatenate([cost_slope, hidden], axis=1).astype(jnp.bfloat16)
    joined_rim = rimmed_field(joined)
    gate_all = conv_three(lstm_weight, joined_rim, "io") + lstm_bias[None, :, None, None]
    in_gate = jax.nn.sigmoid(gate_all[:, :units])
    forget_gate = jax.nn.sigmoid(gate_all[:, units : 2 * units])
    out_gate = jax.nn.sigmoid(gate_all[:, 2 * units : 3 * units])
    update = jnp.tanh(gate_all[:, 3 * units :])
    memory_next = forget_gate * memory + in_gate * update
    squashed = jnp.tanh(memory_next)
    hidden_next = out_gate * squashed
    hidden_low = hidden_next.astype(jnp.bfloat16)
    stepped = jnp.einsum(
        "fh,bhwl->bfwl", out_weight, hidden_low, preferred_element_type=jnp.float32
    )
    saved = (
        state_rim,
        pre_prior,
        latent_rim,
        joined_rim,
        in_gate,
        forget_gate,
        out_gate,
        update,
        memory,
        squashed,
        hidden_low,
    )
    return (current - stepped, hidden_next, memory_next, saved)


def backward(slope_state, slope_hidden, slope_memory, saved, obs_weight, weights, leading):
    prior_in, prior_out, lstm_weight, lstm_bias, out_weight = weights
    (
        state_rim,
        pre_prior,
        latent_rim,
        joined_rim,
        in_gate,
        forget_gate,
        out_gate,
        update,
        memory,
        squashed,
        hidden_low,
    ) = saved
    frames = slope_state.shape[1]
    neg_low = (-slope_state).astype(jnp.bfloat16)
    grad_outw = jnp.einsum("bfwl,bhwl->fh", neg_low, hidden_low, preferred_element_type=jnp.float32)
    slope_hid = (
        jnp.einsum("fh,bfwl->bhwl", out_weight, neg_low, preferred_element_type=jnp.float32)
        + slope_hidden
    )
    slope_mem = slope_hid * out_gate * (1.0 - squashed * squashed) + slope_memory
    gate_slope = jnp.concatenate(
        [
            slope_mem * update * in_gate * (1.0 - in_gate),
            slope_mem * memory * forget_gate * (1.0 - forget_gate),
            slope_hid * squashed * out_gate * (1.0 - out_gate),
            slope_mem * in_gate * (1.0 - update * update),
        ],
        axis=1,
    )
    grad_bias = jnp.sum(gate_slope, axis=(0, 2, 3))
    gate_low = gate_slope.astype(jnp.bfloat16)
    grad_lstm = kernel_slope(gate_low, joined_rim, "io")
    back_kernel = lstm_weight[::-1]
    if leading:
        back_kernel = back_kernel[:, :frames]
    gate_rimmed = padded_2(gate_low, (("band", 2),), 1)
    joined_slope = conv_three(back_kernel, gate_rimmed)
    cost_part = joined_slope[:, :frames]
    hidden_back = None if leading else joined_slope[:, frames:]
    slope_prev = slope_state + (obs_weight + prior_weight) * cost_part
    prior_low = (-prior_weight * cost_part).astype(jnp.bfloat16)
    grad_pout = kernel_slope(prior_low, latent_rim)
    latent_slope = conv_three(flipped(prior_out), padded_2(prior_low, (("band", 2),), 2))
    sigma = jax.nn.sigmoid(pre_prior)
    pre_rim = (latent_slope * (sigma + pre_prior * sigma * (1.0 - sigma))).astype(jnp.bfloat16)
    pre_rim = edge_zeroed(pre_rim)
    grad_pin = kernel_slope(pre_rim[:, :, 1:-1], state_rim)
    slope_prev = slope_prev + conv_three(flipped(prior_in), pre_rim)
    memory_back = slope_mem * forget_gate
    return (
        slope_prev,
        hidden_back,
        memory_back,
        (grad_pin, grad_pout, grad_lstm, grad_bias, grad_outw),
    )


def body(
    first_guess,
    observed_height,
    swath_cells,
    drift_value,
    drift_cell,
    prior_in,
    prior_out,
    lstm_weight,
    lstm_bias,
    out_weight,
    final_slope,
):
    batch, frames, breadth, lat_count = first_guess.shape
    block = breadth * lat_count
    spots = jnp.arange(block, dtype=jnp.int32)
    hits = swath_cells[:, :, 0, :, None] == spots
    mask = jnp.any(hits, axis=2).astype(jnp.float32).reshape(batch, frames, breadth, lat_count)
    packed = jnp.stack([drift_value, drift_cell.astype(jnp.float32)])
    arrived = lax.all_to_all(packed, "band", split_axis=3, concat_axis=2, tiled=True)
    arrived_value = arrived[0].reshape(batch, -1)
    arrived_cell = arrived[1].astype(jnp.int32).reshape(batch, -1)
    places = jnp.arange(frames * block, dtype=jnp.int32).reshape(frames, breadth, lat_count)
    landed = arrived_cell[:, :, None, None, None] == places
    drift_count = jnp.sum(landed.astype(jnp.float32), axis=1)
    drift_total = jnp.sum(jnp.where(landed, arrived_value[:, :, None, None, None], 0.0), axis=1)
    obs_weight = mask + drift_count
    obs_target = mask * observed_height + drift_total
    weights = (prior_in, prior_out, lstm_weight, lstm_bias, out_weight)
    units = out_weight.shape[1]
    blank = jnp.zeros((batch, units, breadth, lat_count), jnp.float32)
    state_one, hid_one, mem_one, saved_one = forward(
        first_guess, blank, blank, obs_weight, obs_target, weights
    )
    state_two, hid_two, mem_two, saved_two = forward(
        state_one, hid_one, mem_one, obs_weight, obs_target, weights
    )
    slope_mid, hidden_back, memory_back, grads_two = backward(
        final_slope, blank, blank, saved_two, obs_weight, weights, False
    )
    slope_start, unused_hid, unused_mem, grads_one = backward(
        slope_mid, hidden_back, memory_back, saved_one, obs_weight, weights, True
    )
    summed = jax.tree.map(jnp.add, grads_one, grads_two)
    cells_all = batch * lax.axis_size("win") * breadth * lax.axis_size("band") * lat_count
    scale = 1.0 / jnp.sqrt(jnp.float32(cells_all))
    grad_pin, grad_pout, grad_lstm, grad_bias, grad_outw = summed
    taps, ins, outs = grad_lstm.shape
    rows = jnp.pad(grad_lstm, ((0, 0), (0, (-ins) % 8), (0, 0))).reshape(-1, outs)
    lstm_total = summed_everywhere(rows, "band", "win")
    lstm_total = lstm_total.reshape(taps, -1, outs)[:, :ins]
    small = [grad_pin, grad_pout, grad_bias, grad_outw]
    flat = jnp.concatenate([member.reshape(-1) for member in small])
    flat = summed_everywhere(flat, "band", "win")
    totals = []
    offset = 0
    for member in small:
        length = member.size
        totals.append(flat[offset : offset + length].reshape(member.shape))
        offset = offset + length
    totals = [totals[0], totals[1], lstm_total, totals[2], totals[3]]
    return (
        slope_start,
        totals[0] * scale,
        totals[1] * scale,
        totals[2] * scale,
        totals[3] * scale,
        totals[4] * scale,
    )


def summed_everywhere(flat, outer, inner):
    bands, wins = lax.axis_size(outer), lax.axis_size(inner)
    count = bands * wins
    if count & (count - 1):
        return lax.psum(flat, (outer, inner))
    axes = (outer, inner)
    inner_bits = wins.bit_length() - 1
    levels = (count.bit_length() - 1)
    order = ([inner_bits] if inner_bits < levels else []) + list(range(inner_bits)) + list(range(inner_bits + 1, levels))
    me = lax.axis_index(axes)
    extent = flat.shape[0]
    cur = jnp.pad(flat, [(0, (-extent) % count)] + [(0, 0)] * (flat.ndim - 1))
    for level in order:
        mask = 1 << level
        half = cur.shape[0] // 2
        high = (me & mask) != 0
        low_part, high_part = cur[:half], cur[half:]
        keep = jnp.where(high, high_part, low_part)
        send = jnp.where(high, low_part, high_part)
        cur = keep + lax.ppermute(send, axes, [(i, i ^ mask) for i in range(count)])
    for level in reversed(order):
        mask = 1 << level
        high = (me & mask) != 0
        other = lax.ppermute(cur, axes, [(i, i ^ mask) for i in range(count)])
        cur = jnp.where(high, jnp.concatenate([other, cur]), jnp.concatenate([cur, other]))
    return cur[:extent]


def solution(mesh):
    return jax.shard_map(
        body,
        mesh=mesh,
        in_specs=(
            P("win", None, "band", None),
            P("win", None, "band", None),
            P("win", None, "band", None),
            P("win", "band", None, None),
            P("win", "band", None, None),
            P(),
            P(),
            P(),
            P(),
            P(),
            P("win", None, "band", None),
        ),
        out_specs=(P("win", None, "band", None), P(), P(), P(), P(), P()),
        check_vma=False,
    )
```

```python
import jax
import jax.numpy as jnp
from jax import lax
from jax.sharding import PartitionSpec as P

prior_weight = 1.0


def padded_2(array, sides, width):
    for axis, dim in sides:
        size, length = (lax.axis_size(axis), array.shape[dim])
        up = [(i, (i + 1) % size) for i in range(size - 1)]
        down = [(j, i) for i, j in up]
        last = lax.slice_in_dim(array, length - width, length, axis=dim)
        first = lax.slice_in_dim(array, 0, width, axis=dim)
        before = lax.ppermute(last, axis, up)
        after = lax.ppermute(first, axis, down)
        array = jnp.concatenate([before, array, after], axis=dim)
    return array


def conv_three(kernel, padded, form="oi"):
    breadth = padded.shape[2] - 2
    lat_count = padded.shape[3]
    framed = jnp.pad(padded, ((0, 0), (0, 0), (0, 0), (1, 1)))
    summed = None
    for lon_off in range(3):
        for lat_off in range(3):
            window = framed[:, :, lon_off : lon_off + breadth, lat_off : lat_off + lat_count]
            contrib = jnp.einsum(
                form + ",biwl->bowl",
                kernel[3 * lon_off + lat_off],
                window,
                preferred_element_type=jnp.float32,
            )
            summed = contrib if summed is None else summed + contrib
    return summed


def kernel_slope(cotangent, padded, form="oi"):
    breadth = cotangent.shape[2]
    lat_count = cotangent.shape[3]
    framed = jnp.pad(padded, ((0, 0), (0, 0), (0, 0), (1, 1)))
    pieces = []
    for lon_off in range(3):
        for lat_off in range(3):
            window = framed[:, :, lon_off : lon_off + breadth, lat_off : lat_off + lat_count]
            pieces.append(
                jnp.einsum(
                    "bowl,biwl->" + form, cotangent, window, preferred_element_type=jnp.float32
                )
            )
    return jnp.stack(pieces)


def flipped(kernel):
    return jnp.transpose(kernel[::-1], (0, 2, 1))


def rimmed_field(field):
    return padded_2(field, (("band", 2),), 1)


def edge_zeroed(field):
    place = lax.axis_index("band")
    last = lax.axis_size("band") - 1
    width = field.shape[2]
    column = lax.broadcasted_iota(jnp.int32, (1, 1, width, 1), 2)
    outside = ((place == 0) & (column == 0)) | ((place == last) & (column == width - 1))
    return jnp.where(outside, jnp.zeros_like(field), field)


def rimmed_slope(field):
    return padded_2(field, (("band", 2),), 1)


def forward(current, hidden, memory, obs_weight, obs_target, weights):
    prior_in, prior_out, lstm_weight, lstm_bias, out_weight = weights
    units = out_weight.shape[1]
    state_wide = padded_2(current.astype(jnp.bfloat16), (("band", 2),), 2)
    state_rim = state_wide[:, :, 1:-1]
    pre_prior = conv_three(prior_in, state_wide)
    latent_rim = edge_zeroed(jax.nn.silu(pre_prior).astype(jnp.bfloat16))
    prior_state = conv_three(prior_out, latent_rim)
    cost_slope = obs_weight * current - obs_target + prior_weight * (current - prior_state)
    joined = jnp.concatenate([cost_slope, hidden], axis=1).astype(jnp.bfloat16)
    joined_rim = rimmed_field(joined)
    gate_all = conv_three(lstm_weight, joined_rim, "io") + lstm_bias[None, :, None, None]
    in_gate = jax.nn.sigmoid(gate_all[:, :units])
    forget_gate = jax.nn.sigmoid(gate_all[:, units : 2 * units])
    out_gate = jax.nn.sigmoid(gate_all[:, 2 * units : 3 * units])
    update = jnp.tanh(gate_all[:, 3 * units :])
    memory_next = forget_gate * memory + in_gate * update
    squashed = jnp.tanh(memory_next)
    hidden_next = out_gate * squashed
    hidden_low = hidden_next.astype(jnp.bfloat16)
    stepped = jnp.einsum(
        "fh,bhwl->bfwl", out_weight, hidden_low, preferred_element_type=jnp.float32
    )
    saved = (
        state_rim,
        pre_prior,
        latent_rim,
        joined_rim,
        in_gate,
        forget_gate,
        out_gate,
        update,
        memory,
        squashed,
        hidden_low,
    )
    return (current - stepped, hidden_next, memory_next, saved)


def backward(slope_state, slope_hidden, slope_memory, saved, obs_weight, weights, leading):
    prior_in, prior_out, lstm_weight, lstm_bias, out_weight = weights
    (
        state_rim,
        pre_prior,
        latent_rim,
        joined_rim,
        in_gate,
        forget_gate,
        out_gate,
        update,
        memory,
        squashed,
        hidden_low,
    ) = saved
    frames = slope_state.shape[1]
    neg_low = (-slope_state).astype(jnp.bfloat16)
    grad_outw = jnp.einsum("bfwl,bhwl->fh", neg_low, hidden_low, preferred_element_type=jnp.float32)
    slope_hid = (
        jnp.einsum("fh,bfwl->bhwl", out_weight, neg_low, preferred_element_type=jnp.float32)
        + slope_hidden
    )
    slope_mem = slope_hid * out_gate * (1.0 - squashed * squashed) + slope_memory
    gate_slope = jnp.concatenate(
        [
            slope_mem * update * in_gate * (1.0 - in_gate),
            slope_mem * memory * forget_gate * (1.0 - forget_gate),
            slope_hid * squashed * out_gate * (1.0 - out_gate),
            slope_mem * in_gate * (1.0 - update * update),
        ],
        axis=1,
    )
    grad_bias = jnp.sum(gate_slope, axis=(0, 2, 3))
    gate_low = gate_slope.astype(jnp.bfloat16)
    grad_lstm = kernel_slope(gate_low, joined_rim, "io")
    back_kernel = lstm_weight[::-1]
    if leading:
        back_kernel = back_kernel[:, :frames]
    gate_rimmed = padded_2(gate_low, (("band", 2),), 1)
    joined_slope = conv_three(back_kernel, gate_rimmed)
    cost_part = joined_slope[:, :frames]
    hidden_back = None if leading else joined_slope[:, frames:]
    slope_prev = slope_state + (obs_weight + prior_weight) * cost_part
    prior_low = (-prior_weight * cost_part).astype(jnp.bfloat16)
    grad_pout = kernel_slope(prior_low, latent_rim)
    latent_slope = conv_three(flipped(prior_out), padded_2(prior_low, (("band", 2),), 2))
    sigma = jax.nn.sigmoid(pre_prior)
    pre_rim = (latent_slope * (sigma + pre_prior * sigma * (1.0 - sigma))).astype(jnp.bfloat16)
    pre_rim = edge_zeroed(pre_rim)
    grad_pin = kernel_slope(pre_rim[:, :, 1:-1], state_rim)
    slope_prev = slope_prev + conv_three(flipped(prior_in), pre_rim)
    memory_back = slope_mem * forget_gate
    return (
        slope_prev,
        hidden_back,
        memory_back,
        (grad_pin, grad_pout, grad_lstm, grad_bias, grad_outw),
    )


def body(
    first_guess,
    observed_height,
    swath_cells,
    drift_value,
    drift_cell,
    prior_in,
    prior_out,
    lstm_weight,
    lstm_bias,
    out_weight,
    final_slope,
):
    batch, frames, breadth, lat_count = first_guess.shape
    block = breadth * lat_count
    spots = jnp.arange(block, dtype=jnp.int32)
    hits = swath_cells[:, :, 0, :, None] == spots
    mask = jnp.any(hits, axis=2).astype(jnp.float32).reshape(batch, frames, breadth, lat_count)
    packed = jnp.stack([drift_value, drift_cell.astype(jnp.float32)])
    arrived = lax.all_to_all(packed, "band", split_axis=3, concat_axis=2, tiled=True)
    arrived_value = arrived[0].reshape(batch, -1)
    arrived_cell = arrived[1].astype(jnp.int32).reshape(batch, -1)
    places = jnp.arange(frames * block, dtype=jnp.int32).reshape(frames, breadth, lat_count)
    landed = arrived_cell[:, :, None, None, None] == places
    drift_count = jnp.sum(landed.astype(jnp.float32), axis=1)
    drift_total = jnp.sum(jnp.where(landed, arrived_value[:, :, None, None, None], 0.0), axis=1)
    obs_weight = mask + drift_count
    obs_target = mask * observed_height + drift_total
    weights = (prior_in, prior_out, lstm_weight, lstm_bias, out_weight)
    units = out_weight.shape[1]
    blank = jnp.zeros((batch, units, breadth, lat_count), jnp.float32)
    state_one, hid_one, mem_one, saved_one = forward(
        first_guess, blank, blank, obs_weight, obs_target, weights
    )
    state_two, hid_two, mem_two, saved_two = forward(
        state_one, hid_one, mem_one, obs_weight, obs_target, weights
    )
    slope_mid, hidden_back, memory_back, grads_two = backward(
        final_slope, blank, blank, saved_two, obs_weight, weights, False
    )
    slope_start, unused_hid, unused_mem, grads_one = backward(
        slope_mid, hidden_back, memory_back, saved_one, obs_weight, weights, True
    )
    summed = jax.tree.map(jnp.add, grads_one, grads_two)
    cells_all = batch * lax.axis_size("win") * breadth * lax.axis_size("band") * lat_count
    scale = 1.0 / jnp.sqrt(jnp.float32(cells_all))
    grad_pin, grad_pout, grad_lstm, grad_bias, grad_outw = summed
    taps, ins, outs = grad_lstm.shape
    rows = jnp.pad(grad_lstm, ((0, 0), (0, (-ins) % 8), (0, 0))).reshape(-1, outs)
    small = [grad_pin, grad_pout, grad_bias, grad_outw]
    flat = jnp.concatenate([member.reshape(-1) for member in small])
    count = lax.axis_size("band") * lax.axis_size("win")
    width = flat.shape[0]
    flat = jnp.pad(flat, (0, (-width) % (count * outs))).reshape(-1, outs)
    lstm_total, flat = summed_pair(rows, flat, "band", "win")
    lstm_total = lstm_total.reshape(taps, -1, outs)[:, :ins]
    flat = flat.reshape(-1)[:width]
    totals = []
    offset = 0
    for member in small:
        length = member.size
        totals.append(flat[offset : offset + length].reshape(member.shape))
        offset = offset + length
    totals = [totals[0], totals[1], lstm_total, totals[2], totals[3]]
    return (
        slope_start,
        totals[0] * scale,
        totals[1] * scale,
        totals[2] * scale,
        totals[3] * scale,
        totals[4] * scale,
    )


def summed_everywhere(flat, outer, inner):
    bands, wins = lax.axis_size(outer), lax.axis_size(inner)
    count = bands * wins
    if count & (count - 1):
        return lax.psum(flat, (outer, inner))
    axes = (outer, inner)
    inner_bits = wins.bit_length() - 1
    levels = (count.bit_length() - 1)
    order = ([inner_bits] if inner_bits < levels else []) + list(range(inner_bits)) + list(range(inner_bits + 1, levels))
    me = lax.axis_index(axes)
    extent = flat.shape[0]
    cur = jnp.pad(flat, [(0, (-extent) % count)] + [(0, 0)] * (flat.ndim - 1))
    for level in order:
        mask = 1 << level
        half = cur.shape[0] // 2
        high = (me & mask) != 0
        low_part, high_part = cur[:half], cur[half:]
        keep = jnp.where(high, high_part, low_part)
        send = jnp.where(high, low_part, high_part)
        cur = keep + lax.ppermute(send, axes, [(i, i ^ mask) for i in range(count)])
    for level in reversed(order):
        mask = 1 << level
        high = (me & mask) != 0
        other = lax.ppermute(cur, axes, [(i, i ^ mask) for i in range(count)])
        cur = jnp.where(high, jnp.concatenate([other, cur]), jnp.concatenate([cur, other]))
    return cur[:extent]


def summed_pair(big, small, outer, inner):
    bands, wins = lax.axis_size(outer), lax.axis_size(inner)
    count = bands * wins
    if count & (count - 1):
        return lax.psum(big, (outer, inner)), lax.psum(small, (outer, inner))
    axes = (outer, inner)
    inner_bits = wins.bit_length() - 1
    levels = count.bit_length() - 1
    order = ([inner_bits] if inner_bits < levels else []) + list(range(inner_bits)) + list(range(inner_bits + 1, levels))
    me = lax.axis_index(axes)

    def halved(cur):
        for level in order:
            mask = 1 << level
            half = cur.shape[0] // 2
            high = (me & mask) != 0
            low_part, high_part = cur[:half], cur[half:]
            keep = jnp.where(high, high_part, low_part)
            send = jnp.where(high, low_part, high_part)
            cur = keep + lax.ppermute(send, axes, [(i, i ^ mask) for i in range(count)])
        return cur

    extent = big.shape[0]
    big_part = halved(jnp.pad(big, [(0, (-extent) % count)] + [(0, 0)] * (big.ndim - 1)))
    small_part = halved(small)
    cur = jnp.concatenate([big_part, small_part])
    for level in reversed(order):
        mask = 1 << level
        high = (me & mask) != 0
        other = lax.ppermute(cur, axes, [(i, i ^ mask) for i in range(count)])
        cur = jnp.where(high, jnp.concatenate([other, cur]), jnp.concatenate([cur, other]))
    cur = cur.reshape((count, -1) + cur.shape[1:])
    split = big_part.shape[0]
    whole_big = cur[:, :split].reshape((-1,) + cur.shape[2:])[:extent]
    whole_small = cur[:, split:].reshape((-1,) + cur.shape[2:])
    return whole_big, whole_small


def solution(mesh):
    return jax.shard_map(
        body,
        mesh=mesh,
        in_specs=(
            P("win", None, "band", None),
            P("win", None, "band", None),
            P("win", None, "band", None),
            P("win", "band", None, None),
            P("win", "band", None, None),
            P(),
            P(),
            P(),
            P(),
            P(),
            P("win", None, "band", None),
        ),
        out_specs=(P("win", None, "band", None), P(), P(), P(), P(), P()),
        check_vma=False,
    )
```

```python
import jax
import jax.numpy as jnp
from jax import lax
from jax.sharding import PartitionSpec as P

prior_weight = 1.0


def padded_2(array, sides, width):
    for axis, dim in sides:
        size, length = (lax.axis_size(axis), array.shape[dim])
        up = [(i, (i + 1) % size) for i in range(size - 1)]
        down = [(j, i) for i, j in up]
        last = lax.slice_in_dim(array, length - width, length, axis=dim)
        first = lax.slice_in_dim(array, 0, width, axis=dim)
        before = lax.ppermute(last, axis, up)
        after = lax.ppermute(first, axis, down)
        array = jnp.concatenate([before, array, after], axis=dim)
    return array


def conv_three(kernel, padded, form="oi"):
    breadth = padded.shape[2] - 2
    lat_count = padded.shape[3]
    framed = jnp.pad(padded, ((0, 0), (0, 0), (0, 0), (1, 1)))
    summed = None
    for lon_off in range(3):
        for lat_off in range(3):
            window = framed[:, :, lon_off : lon_off + breadth, lat_off : lat_off + lat_count]
            contrib = jnp.einsum(
                form + ",biwl->bowl",
                kernel[3 * lon_off + lat_off],
                window,
                preferred_element_type=jnp.float32,
            )
            summed = contrib if summed is None else summed + contrib
    return summed


def kernel_slope(cotangent, padded, form="oi"):
    breadth = cotangent.shape[2]
    lat_count = cotangent.shape[3]
    framed = jnp.pad(padded, ((0, 0), (0, 0), (0, 0), (1, 1)))
    pieces = []
    for lon_off in range(3):
        for lat_off in range(3):
            window = framed[:, :, lon_off : lon_off + breadth, lat_off : lat_off + lat_count]
            pieces.append(
                jnp.einsum(
                    "bowl,biwl->" + form, cotangent, window, preferred_element_type=jnp.float32
                )
            )
    return jnp.stack(pieces)


def flipped(kernel):
    return jnp.transpose(kernel[::-1], (0, 2, 1))


def rimmed_field(field):
    return padded_2(field, (("band", 2),), 1)


def edge_zeroed(field, depth=1):
    place = lax.axis_index("band")
    last = lax.axis_size("band") - 1
    width = field.shape[2]
    column = lax.broadcasted_iota(jnp.int32, (1, 1, width, 1), 2)
    outside = ((place == 0) & (column < depth)) | ((place == last) & (column >= width - depth))
    return jnp.where(outside, jnp.zeros_like(field), field)


def rimmed_slope(field):
    return padded_2(field, (("band", 2),), 1)


def forward(current, hidden, memory, obs_weight, obs_target, weights):
    prior_in, prior_out, lstm_weight, lstm_bias, out_weight = weights
    units = out_weight.shape[1]
    state_wide = padded_2(current.astype(jnp.bfloat16), (("band", 2),), 2)
    state_rim = state_wide[:, :, 1:-1]
    pre_prior = conv_three(prior_in, state_wide)
    latent_rim = edge_zeroed(jax.nn.silu(pre_prior).astype(jnp.bfloat16))
    prior_state = conv_three(prior_out, latent_rim)
    cost_slope = obs_weight * current - obs_target + prior_weight * (current - prior_state)
    joined = jnp.concatenate([cost_slope, hidden], axis=1).astype(jnp.bfloat16)
    joined_rim = rimmed_field(joined)
    return lstm_tail(current, memory, state_rim, pre_prior, latent_rim, joined_rim, weights)

def forward_first(current, obs_weight, obs_target, weights):
    prior_in, prior_out, lstm_weight, lstm_bias, out_weight = weights
    units = out_weight.shape[1]
    frames = current.shape[1]
    batch, _, breadth, lat_count = current.shape
    fields = jnp.concatenate([current, obs_weight, obs_target], axis=1)
    wide = padded_2(fields, (("band", 2),), 3)
    current_wide = wide[:, :frames]
    state_wide = current_wide.astype(jnp.bfloat16)
    pre_wide = conv_three(prior_in, state_wide)
    latent_wide = edge_zeroed(jax.nn.silu(pre_wide).astype(jnp.bfloat16), 2)
    prior_state = conv_three(prior_out, latent_wide)
    near = wide[:, :, 2:-2]
    here, weight_near, target_near = near[:, :frames], near[:, frames : 2 * frames], near[:, 2 * frames :]
    cost_slope = weight_near * here - target_near + prior_weight * (here - prior_state)
    hidden_near = jnp.zeros((batch, units, breadth + 2, lat_count), jnp.float32)
    joined_rim = edge_zeroed(jnp.concatenate([cost_slope, hidden_near], axis=1).astype(jnp.bfloat16))
    memory = jnp.zeros((batch, units, breadth, lat_count), jnp.float32)
    state_rim = state_wide[:, :, 2:-2]
    pre_prior = pre_wide[:, :, 1:-1]
    latent_rim = latent_wide[:, :, 1:-1]
    return lstm_tail(current, memory, state_rim, pre_prior, latent_rim, joined_rim, weights)


def lstm_tail(current, memory, state_rim, pre_prior, latent_rim, joined_rim, weights):
    prior_in, prior_out, lstm_weight, lstm_bias, out_weight = weights
    units = out_weight.shape[1]
    gate_all = conv_three(lstm_weight, joined_rim, "io") + lstm_bias[None, :, None, None]
    in_gate = jax.nn.sigmoid(gate_all[:, :units])
    forget_gate = jax.nn.sigmoid(gate_all[:, units : 2 * units])
    out_gate = jax.nn.sigmoid(gate_all[:, 2 * units : 3 * units])
    update = jnp.tanh(gate_all[:, 3 * units :])
    memory_next = forget_gate * memory + in_gate * update
    squashed = jnp.tanh(memory_next)
    hidden_next = out_gate * squashed
    hidden_low = hidden_next.astype(jnp.bfloat16)
    stepped = jnp.einsum(
        "fh,bhwl->bfwl", out_weight, hidden_low, preferred_element_type=jnp.float32
    )
    saved = (
        state_rim,
        pre_prior,
        latent_rim,
        joined_rim,
        in_gate,
        forget_gate,
        out_gate,
        update,
        memory,
        squashed,
        hidden_low,
    )
    return (current - stepped, hidden_next, memory_next, saved)


def backward(slope_state, slope_hidden, slope_memory, saved, obs_weight, weights, leading):
    prior_in, prior_out, lstm_weight, lstm_bias, out_weight = weights
    (
        state_rim,
        pre_prior,
        latent_rim,
        joined_rim,
        in_gate,
        forget_gate,
        out_gate,
        update,
        memory,
        squashed,
        hidden_low,
    ) = saved
    frames = slope_state.shape[1]
    neg_low = (-slope_state).astype(jnp.bfloat16)
    grad_outw = jnp.einsum("bfwl,bhwl->fh", neg_low, hidden_low, preferred_element_type=jnp.float32)
    slope_hid = (
        jnp.einsum("fh,bfwl->bhwl", out_weight, neg_low, preferred_element_type=jnp.float32)
        + slope_hidden
    )
    slope_mem = slope_hid * out_gate * (1.0 - squashed * squashed) + slope_memory
    gate_slope = jnp.concatenate(
        [
            slope_mem * update * in_gate * (1.0 - in_gate),
            slope_mem * memory * forget_gate * (1.0 - forget_gate),
            slope_hid * squashed * out_gate * (1.0 - out_gate),
            slope_mem * in_gate * (1.0 - update * update),
        ],
        axis=1,
    )
    grad_bias = jnp.sum(gate_slope, axis=(0, 2, 3))
    gate_low = gate_slope.astype(jnp.bfloat16)
    grad_lstm = kernel_slope(gate_low, joined_rim, "io")
    back_kernel = lstm_weight[::-1]
    if leading:
        back_kernel = back_kernel[:, :frames]
    gate_rimmed = padded_2(gate_low, (("band", 2),), 1)
    joined_slope = conv_three(back_kernel, gate_rimmed)
    cost_part = joined_slope[:, :frames]
    hidden_back = None if leading else joined_slope[:, frames:]
    slope_prev = slope_state + (obs_weight + prior_weight) * cost_part
    prior_low = (-prior_weight * cost_part).astype(jnp.bfloat16)
    grad_pout = kernel_slope(prior_low, latent_rim)
    latent_slope = conv_three(flipped(prior_out), padded_2(prior_low, (("band", 2),), 2))
    sigma = jax.nn.sigmoid(pre_prior)
    pre_rim = (latent_slope * (sigma + pre_prior * sigma * (1.0 - sigma))).astype(jnp.bfloat16)
    pre_rim = edge_zeroed(pre_rim)
    grad_pin = kernel_slope(pre_rim[:, :, 1:-1], state_rim)
    slope_prev = slope_prev + conv_three(flipped(prior_in), pre_rim)
    memory_back = slope_mem * forget_gate
    return (
        slope_prev,
        hidden_back,
        memory_back,
        (grad_pin, grad_pout, grad_lstm, grad_bias, grad_outw),
    )


def body(
    first_guess,
    observed_height,
    swath_cells,
    drift_value,
    drift_cell,
    prior_in,
    prior_out,
    lstm_weight,
    lstm_bias,
    out_weight,
    final_slope,
):
    batch, frames, breadth, lat_count = first_guess.shape
    block = breadth * lat_count
    spots = jnp.arange(block, dtype=jnp.int32)
    hits = swath_cells[:, :, 0, :, None] == spots
    mask = jnp.any(hits, axis=2).astype(jnp.float32).reshape(batch, frames, breadth, lat_count)
    packed = jnp.stack([drift_value, drift_cell.astype(jnp.float32)])
    arrived = lax.all_to_all(packed, "band", split_axis=3, concat_axis=2, tiled=True)
    arrived_value = arrived[0].reshape(batch, -1)
    arrived_cell = arrived[1].astype(jnp.int32).reshape(batch, -1)
    places = jnp.arange(frames * block, dtype=jnp.int32).reshape(frames, breadth, lat_count)
    landed = arrived_cell[:, :, None, None, None] == places
    drift_count = jnp.sum(landed.astype(jnp.float32), axis=1)
    drift_total = jnp.sum(jnp.where(landed, arrived_value[:, :, None, None, None], 0.0), axis=1)
    obs_weight = mask + drift_count
    obs_target = mask * observed_height + drift_total
    weights = (prior_in, prior_out, lstm_weight, lstm_bias, out_weight)
    units = out_weight.shape[1]
    blank = jnp.zeros((batch, units, breadth, lat_count), jnp.float32)
    state_one, hid_one, mem_one, saved_one = forward_first(first_guess, obs_weight, obs_target, weights)
    state_two, hid_two, mem_two, saved_two = forward(
        state_one, hid_one, mem_one, obs_weight, obs_target, weights
    )
    slope_mid, hidden_back, memory_back, grads_two = backward(
        final_slope, blank, blank, saved_two, obs_weight, weights, False
    )
    slope_start, unused_hid, unused_mem, grads_one = backward(
        slope_mid, hidden_back, memory_back, saved_one, obs_weight, weights, True
    )
    summed = jax.tree.map(jnp.add, grads_one, grads_two)
    cells_all = batch * lax.axis_size("win") * breadth * lax.axis_size("band") * lat_count
    scale = 1.0 / jnp.sqrt(jnp.float32(cells_all))
    grad_pin, grad_pout, grad_lstm, grad_bias, grad_outw = summed
    taps, ins, outs = grad_lstm.shape
    rows = jnp.pad(grad_lstm, ((0, 0), (0, (-ins) % 8), (0, 0))).reshape(-1, outs)
    lstm_total = summed_everywhere(rows, "band", "win")
    lstm_total = lstm_total.reshape(taps, -1, outs)[:, :ins]
    small = [grad_pin, grad_pout, grad_bias, grad_outw]
    flat = jnp.concatenate([member.reshape(-1) for member in small])
    flat = summed_everywhere(flat, "band", "win")
    totals = []
    offset = 0
    for member in small:
        length = member.size
        totals.append(flat[offset : offset + length].reshape(member.shape))
        offset = offset + length
    totals = [totals[0], totals[1], lstm_total, totals[2], totals[3]]
    return (
        slope_start,
        totals[0] * scale,
        totals[1] * scale,
        totals[2] * scale,
        totals[3] * scale,
        totals[4] * scale,
    )


def summed_everywhere(flat, outer, inner):
    bands, wins = lax.axis_size(outer), lax.axis_size(inner)
    count = bands * wins
    if count & (count - 1):
        return lax.psum(flat, (outer, inner))
    axes = (outer, inner)
    inner_bits = wins.bit_length() - 1
    levels = (count.bit_length() - 1)
    order = ([inner_bits] if inner_bits < levels else []) + list(range(inner_bits)) + list(range(inner_bits + 1, levels))
    me = lax.axis_index(axes)
    extent = flat.shape[0]
    cur = jnp.pad(flat, [(0, (-extent) % count)] + [(0, 0)] * (flat.ndim - 1))
    for level in order:
        mask = 1 << level
        half = cur.shape[0] // 2
        high = (me & mask) != 0
        low_part, high_part = cur[:half], cur[half:]
        keep = jnp.where(high, high_part, low_part)
        send = jnp.where(high, low_part, high_part)
        cur = keep + lax.ppermute(send, axes, [(i, i ^ mask) for i in range(count)])
    for level in reversed(order):
        mask = 1 << level
        high = (me & mask) != 0
        other = lax.ppermute(cur, axes, [(i, i ^ mask) for i in range(count)])
        cur = jnp.where(high, jnp.concatenate([other, cur]), jnp.concatenate([cur, other]))
    return cur[:extent]


def solution(mesh):
    return jax.shard_map(
        body,
        mesh=mesh,
        in_specs=(
            P("win", None, "band", None),
            P("win", None, "band", None),
            P("win", None, "band", None),
            P("win", "band", None, None),
            P("win", "band", None, None),
            P(),
            P(),
            P(),
            P(),
            P(),
            P("win", None, "band", None),
        ),
        out_specs=(P("win", None, "band", None), P(), P(), P(), P(), P()),
        check_vma=False,
    )
```

```python
import jax
import jax.numpy as jnp
from jax import lax
from jax.sharding import PartitionSpec as P

prior_weight = 1.0


def padded_2(array, sides, width):
    for axis, dim in sides:
        size, length = (lax.axis_size(axis), array.shape[dim])
        up = [(i, (i + 1) % size) for i in range(size - 1)]
        down = [(j, i) for i, j in up]
        last = lax.slice_in_dim(array, length - width, length, axis=dim)
        first = lax.slice_in_dim(array, 0, width, axis=dim)
        before = lax.ppermute(last, axis, up)
        after = lax.ppermute(first, axis, down)
        array = jnp.concatenate([before, array, after], axis=dim)
    return array


def conv_three(kernel, padded, form="oi"):
    breadth = padded.shape[2] - 2
    lat_count = padded.shape[3]
    framed = jnp.pad(padded, ((0, 0), (0, 0), (0, 0), (1, 1)))
    summed = None
    for lon_off in range(3):
        for lat_off in range(3):
            window = framed[:, :, lon_off : lon_off + breadth, lat_off : lat_off + lat_count]
            contrib = jnp.einsum(
                form + ",biwl->bowl",
                kernel[3 * lon_off + lat_off],
                window,
                preferred_element_type=jnp.float32,
            )
            summed = contrib if summed is None else summed + contrib
    return summed


def kernel_slope(cotangent, padded, form="oi"):
    breadth = cotangent.shape[2]
    lat_count = cotangent.shape[3]
    framed = jnp.pad(padded, ((0, 0), (0, 0), (0, 0), (1, 1)))
    pieces = []
    for lon_off in range(3):
        for lat_off in range(3):
            window = framed[:, :, lon_off : lon_off + breadth, lat_off : lat_off + lat_count]
            pieces.append(
                jnp.einsum(
                    "bowl,biwl->" + form, cotangent, window, preferred_element_type=jnp.float32
                )
            )
    return jnp.stack(pieces)


def flipped(kernel):
    return jnp.transpose(kernel[::-1], (0, 2, 1))


def rimmed_field(field):
    return padded_2(field, (("band", 2),), 1)


def edge_zeroed(field, depth=1):
    place = lax.axis_index("band")
    last = lax.axis_size("band") - 1
    width = field.shape[2]
    column = lax.broadcasted_iota(jnp.int32, (1, 1, width, 1), 2)
    outside = ((place == 0) & (column < depth)) | ((place == last) & (column >= width - depth))
    return jnp.where(outside, jnp.zeros_like(field), field)


def rimmed_slope(field):
    return padded_2(field, (("band", 2),), 1)


def forward(current, hidden, memory, obs_weight, obs_target, weights):
    prior_in, prior_out, lstm_weight, lstm_bias, out_weight = weights
    units = out_weight.shape[1]
    state_wide = padded_2(current.astype(jnp.bfloat16), (("band", 2),), 2)
    state_rim = state_wide[:, :, 1:-1]
    pre_prior = conv_three(prior_in, state_wide)
    latent_rim = edge_zeroed(jax.nn.silu(pre_prior).astype(jnp.bfloat16))
    prior_state = conv_three(prior_out, latent_rim)
    cost_slope = obs_weight * current - obs_target + prior_weight * (current - prior_state)
    joined = jnp.concatenate([cost_slope, hidden], axis=1).astype(jnp.bfloat16)
    joined_rim = rimmed_field(joined)
    return lstm_tail(current, memory, state_rim, pre_prior, latent_rim, joined_rim, weights)

def forward_first(current, obs_weight, obs_target, weights):
    prior_in, prior_out, lstm_weight, lstm_bias, out_weight = weights
    units = out_weight.shape[1]
    frames = current.shape[1]
    batch, _, breadth, lat_count = current.shape
    fields = jnp.concatenate([current, obs_weight, obs_target], axis=1)
    wide = padded_2(fields, (("band", 2),), 3)
    current_wide = wide[:, :frames]
    state_wide = current_wide.astype(jnp.bfloat16)
    pre_wide = conv_three(prior_in, state_wide)
    latent_wide = edge_zeroed(jax.nn.silu(pre_wide).astype(jnp.bfloat16), 2)
    prior_state = conv_three(prior_out, latent_wide)
    near = wide[:, :, 2:-2]
    here, weight_near, target_near = near[:, :frames], near[:, frames : 2 * frames], near[:, 2 * frames :]
    cost_slope = weight_near * here - target_near + prior_weight * (here - prior_state)
    hidden_near = jnp.zeros((batch, units, breadth + 2, lat_count), jnp.float32)
    joined_rim = edge_zeroed(jnp.concatenate([cost_slope, hidden_near], axis=1).astype(jnp.bfloat16))
    memory = jnp.zeros((batch, units, breadth, lat_count), jnp.float32)
    state_rim = state_wide[:, :, 2:-2]
    pre_prior = pre_wide[:, :, 1:-1]
    latent_rim = latent_wide[:, :, 1:-1]
    stepped = lstm_tail(current, memory, state_rim, pre_prior, latent_rim, joined_rim, weights)
    return stepped + ((weight_near, target_near),)


def edges_swapped(current, hidden_low, reach):
    batch, frames, breadth, lat_count = current.shape
    units = hidden_low.shape[1]
    size = lax.axis_size("band")
    up = [(i, (i + 1) % size) for i in range(size - 1)]
    down = [(j, i) for i, j in up]
    hidden_wide = hidden_low.astype(jnp.float32)

    def packed(state_part, hidden_part):
        return jnp.concatenate([state_part.reshape(batch, -1), hidden_part.reshape(batch, -1)], axis=1)

    before = lax.ppermute(packed(current[:, :, -reach:], hidden_wide[:, :, -1:]), "band", up)
    after = lax.ppermute(packed(current[:, :, :reach], hidden_wide[:, :, :1]), "band", down)
    cut = frames * reach * lat_count

    def unpacked(flat):
        return flat[:, :cut].reshape(batch, frames, reach, lat_count), flat[:, cut:].reshape(batch, units, 1, lat_count)

    state_before, hidden_before = unpacked(before)
    state_after, hidden_after = unpacked(after)
    state_wide = jnp.concatenate([state_before, current, state_after], axis=2)
    hidden_rim = jnp.concatenate([hidden_before, hidden_wide, hidden_after], axis=2)
    return state_wide, hidden_rim


def forward_next(current, hidden, memory, near_fields, weights):
    prior_in, prior_out, lstm_weight, lstm_bias, out_weight = weights
    weight_near, target_near = near_fields
    hidden_low = hidden.astype(jnp.bfloat16)
    current_wide, hidden_rim = edges_swapped(current, hidden_low, 3)
    state_wide = current_wide.astype(jnp.bfloat16)
    pre_wide = conv_three(prior_in, state_wide)
    latent_wide = edge_zeroed(jax.nn.silu(pre_wide).astype(jnp.bfloat16), 2)
    prior_state = conv_three(prior_out, latent_wide)
    here = current_wide[:, :, 2:-2]
    cost_slope = weight_near * here - target_near + prior_weight * (here - prior_state)
    joined_rim = edge_zeroed(jnp.concatenate([cost_slope, hidden_rim], axis=1).astype(jnp.bfloat16))
    state_rim = state_wide[:, :, 2:-2]
    pre_prior = pre_wide[:, :, 1:-1]
    latent_rim = latent_wide[:, :, 1:-1]
    return lstm_tail(current, memory, state_rim, pre_prior, latent_rim, joined_rim, weights)


def lstm_tail(current, memory, state_rim, pre_prior, latent_rim, joined_rim, weights):
    prior_in, prior_out, lstm_weight, lstm_bias, out_weight = weights
    units = out_weight.shape[1]
    gate_all = conv_three(lstm_weight, joined_rim, "io") + lstm_bias[None, :, None, None]
    in_gate = jax.nn.sigmoid(gate_all[:, :units])
    forget_gate = jax.nn.sigmoid(gate_all[:, units : 2 * units])
    out_gate = jax.nn.sigmoid(gate_all[:, 2 * units : 3 * units])
    update = jnp.tanh(gate_all[:, 3 * units :])
    memory_next = forget_gate * memory + in_gate * update
    squashed = jnp.tanh(memory_next)
    hidden_next = out_gate * squashed
    hidden_low = hidden_next.astype(jnp.bfloat16)
    stepped = jnp.einsum(
        "fh,bhwl->bfwl", out_weight, hidden_low, preferred_element_type=jnp.float32
    )
    saved = (
        state_rim,
        pre_prior,
        latent_rim,
        joined_rim,
        in_gate,
        forget_gate,
        out_gate,
        update,
        memory,
        squashed,
        hidden_low,
    )
    return (current - stepped, hidden_next, memory_next, saved)


def backward(slope_state, slope_hidden, slope_memory, saved, obs_weight, weights, leading):
    prior_in, prior_out, lstm_weight, lstm_bias, out_weight = weights
    (
        state_rim,
        pre_prior,
        latent_rim,
        joined_rim,
        in_gate,
        forget_gate,
        out_gate,
        update,
        memory,
        squashed,
        hidden_low,
    ) = saved
    frames = slope_state.shape[1]
    neg_low = (-slope_state).astype(jnp.bfloat16)
    grad_outw = jnp.einsum("bfwl,bhwl->fh", neg_low, hidden_low, preferred_element_type=jnp.float32)
    slope_hid = (
        jnp.einsum("fh,bfwl->bhwl", out_weight, neg_low, preferred_element_type=jnp.float32)
        + slope_hidden
    )
    slope_mem = slope_hid * out_gate * (1.0 - squashed * squashed) + slope_memory
    gate_slope = jnp.concatenate(
        [
            slope_mem * update * in_gate * (1.0 - in_gate),
            slope_mem * memory * forget_gate * (1.0 - forget_gate),
            slope_hid * squashed * out_gate * (1.0 - out_gate),
            slope_mem * in_gate * (1.0 - update * update),
        ],
        axis=1,
    )
    grad_bias = jnp.sum(gate_slope, axis=(0, 2, 3))
    gate_low = gate_slope.astype(jnp.bfloat16)
    grad_lstm = kernel_slope(gate_low, joined_rim, "io")
    back_kernel = lstm_weight[::-1]
    if leading:
        back_kernel = back_kernel[:, :frames]
    gate_rimmed = padded_2(gate_low, (("band", 2),), 1)
    joined_slope = conv_three(back_kernel, gate_rimmed)
    cost_part = joined_slope[:, :frames]
    hidden_back = None if leading else joined_slope[:, frames:]
    slope_prev = slope_state + (obs_weight + prior_weight) * cost_part
    prior_low = (-prior_weight * cost_part).astype(jnp.bfloat16)
    grad_pout = kernel_slope(prior_low, latent_rim)
    latent_slope = conv_three(flipped(prior_out), padded_2(prior_low, (("band", 2),), 2))
    sigma = jax.nn.sigmoid(pre_prior)
    pre_rim = (latent_slope * (sigma + pre_prior * sigma * (1.0 - sigma))).astype(jnp.bfloat16)
    pre_rim = edge_zeroed(pre_rim)
    grad_pin = kernel_slope(pre_rim[:, :, 1:-1], state_rim)
    slope_prev = slope_prev + conv_three(flipped(prior_in), pre_rim)
    memory_back = slope_mem * forget_gate
    return (
        slope_prev,
        hidden_back,
        memory_back,
        (grad_pin, grad_pout, grad_lstm, grad_bias, grad_outw),
    )


def body(
    first_guess,
    observed_height,
    swath_cells,
    drift_value,
    drift_cell,
    prior_in,
    prior_out,
    lstm_weight,
    lstm_bias,
    out_weight,
    final_slope,
):
    batch, frames, breadth, lat_count = first_guess.shape
    block = breadth * lat_count
    spots = jnp.arange(block, dtype=jnp.int32)
    hits = swath_cells[:, :, 0, :, None] == spots
    mask = jnp.any(hits, axis=2).astype(jnp.float32).reshape(batch, frames, breadth, lat_count)
    packed = jnp.stack([drift_value, drift_cell.astype(jnp.float32)])
    arrived = lax.all_to_all(packed, "band", split_axis=3, concat_axis=2, tiled=True)
    arrived_value = arrived[0].reshape(batch, -1)
    arrived_cell = arrived[1].astype(jnp.int32).reshape(batch, -1)
    places = jnp.arange(frames * block, dtype=jnp.int32).reshape(frames, breadth, lat_count)
    landed = arrived_cell[:, :, None, None, None] == places
    drift_count = jnp.sum(landed.astype(jnp.float32), axis=1)
    drift_total = jnp.sum(jnp.where(landed, arrived_value[:, :, None, None, None], 0.0), axis=1)
    obs_weight = mask + drift_count
    obs_target = mask * observed_height + drift_total
    weights = (prior_in, prior_out, lstm_weight, lstm_bias, out_weight)
    units = out_weight.shape[1]
    blank = jnp.zeros((batch, units, breadth, lat_count), jnp.float32)
    state_one, hid_one, mem_one, saved_one, near_fields = forward_first(
        first_guess, obs_weight, obs_target, weights
    )
    state_two, hid_two, mem_two, saved_two = forward_next(
        state_one, hid_one, mem_one, near_fields, weights
    )
    slope_mid, hidden_back, memory_back, grads_two = backward(
        final_slope, blank, blank, saved_two, obs_weight, weights, False
    )
    slope_start, unused_hid, unused_mem, grads_one = backward(
        slope_mid, hidden_back, memory_back, saved_one, obs_weight, weights, True
    )
    summed = jax.tree.map(jnp.add, grads_one, grads_two)
    cells_all = batch * lax.axis_size("win") * breadth * lax.axis_size("band") * lat_count
    scale = 1.0 / jnp.sqrt(jnp.float32(cells_all))
    grad_pin, grad_pout, grad_lstm, grad_bias, grad_outw = summed
    taps, ins, outs = grad_lstm.shape
    rows = jnp.pad(grad_lstm, ((0, 0), (0, (-ins) % 8), (0, 0))).reshape(-1, outs)
    lstm_total = summed_everywhere(rows, "band", "win")
    lstm_total = lstm_total.reshape(taps, -1, outs)[:, :ins]
    small = [grad_pin, grad_pout, grad_bias, grad_outw]
    flat = jnp.concatenate([member.reshape(-1) for member in small])
    flat = summed_everywhere(flat, "band", "win")
    totals = []
    offset = 0
    for member in small:
        length = member.size
        totals.append(flat[offset : offset + length].reshape(member.shape))
        offset = offset + length
    totals = [totals[0], totals[1], lstm_total, totals[2], totals[3]]
    return (
        slope_start,
        totals[0] * scale,
        totals[1] * scale,
        totals[2] * scale,
        totals[3] * scale,
        totals[4] * scale,
    )


def summed_everywhere(flat, outer, inner):
    bands, wins = lax.axis_size(outer), lax.axis_size(inner)
    count = bands * wins
    if count & (count - 1):
        return lax.psum(flat, (outer, inner))
    axes = (outer, inner)
    inner_bits = wins.bit_length() - 1
    levels = (count.bit_length() - 1)
    order = ([inner_bits] if inner_bits < levels else []) + list(range(inner_bits)) + list(range(inner_bits + 1, levels))
    me = lax.axis_index(axes)
    extent = flat.shape[0]
    cur = jnp.pad(flat, [(0, (-extent) % count)] + [(0, 0)] * (flat.ndim - 1))
    for level in order:
        mask = 1 << level
        half = cur.shape[0] // 2
        high = (me & mask) != 0
        low_part, high_part = cur[:half], cur[half:]
        keep = jnp.where(high, high_part, low_part)
        send = jnp.where(high, low_part, high_part)
        cur = keep + lax.ppermute(send, axes, [(i, i ^ mask) for i in range(count)])
    for level in reversed(order):
        mask = 1 << level
        high = (me & mask) != 0
        other = lax.ppermute(cur, axes, [(i, i ^ mask) for i in range(count)])
        cur = jnp.where(high, jnp.concatenate([other, cur]), jnp.concatenate([cur, other]))
    return cur[:extent]


def solution(mesh):
    return jax.shard_map(
        body,
        mesh=mesh,
        in_specs=(
            P("win", None, "band", None),
            P("win", None, "band", None),
            P("win", None, "band", None),
            P("win", "band", None, None),
            P("win", "band", None, None),
            P(),
            P(),
            P(),
            P(),
            P(),
            P("win", None, "band", None),
        ),
        out_specs=(P("win", None, "band", None), P(), P(), P(), P(), P()),
        check_vma=False,
    )
```

```python
import jax
import jax.numpy as jnp
from jax import lax
from jax.sharding import PartitionSpec as P

prior_weight = 1.0


def padded_2(array, sides, width):
    for axis, dim in sides:
        size, length = (lax.axis_size(axis), array.shape[dim])
        up = [(i, (i + 1) % size) for i in range(size - 1)]
        down = [(j, i) for i, j in up]
        last = lax.slice_in_dim(array, length - width, length, axis=dim)
        first = lax.slice_in_dim(array, 0, width, axis=dim)
        before = lax.ppermute(last, axis, up)
        after = lax.ppermute(first, axis, down)
        array = jnp.concatenate([before, array, after], axis=dim)
    return array


def conv_three(kernel, padded, form="oi"):
    breadth = padded.shape[2] - 2
    lat_count = padded.shape[3]
    framed = jnp.pad(padded, ((0, 0), (0, 0), (0, 0), (1, 1)))
    summed = None
    for lon_off in range(3):
        for lat_off in range(3):
            window = framed[:, :, lon_off : lon_off + breadth, lat_off : lat_off + lat_count]
            contrib = jnp.einsum(
                form + ",biwl->bowl",
                kernel[3 * lon_off + lat_off],
                window,
                preferred_element_type=jnp.float32,
            )
            summed = contrib if summed is None else summed + contrib
    return summed


def kernel_slope(cotangent, padded, form="oi"):
    breadth = cotangent.shape[2]
    lat_count = cotangent.shape[3]
    framed = jnp.pad(padded, ((0, 0), (0, 0), (0, 0), (1, 1)))
    pieces = []
    for lon_off in range(3):
        for lat_off in range(3):
            window = framed[:, :, lon_off : lon_off + breadth, lat_off : lat_off + lat_count]
            pieces.append(
                jnp.einsum(
                    "bowl,biwl->" + form, cotangent, window, preferred_element_type=jnp.float32
                )
            )
    return jnp.stack(pieces)


def flipped(kernel):
    return jnp.transpose(kernel[::-1], (0, 2, 1))


def rimmed_field(field):
    return padded_2(field, (("band", 2),), 1)


def edge_zeroed(field, depth=1):
    place = lax.axis_index("band")
    last = lax.axis_size("band") - 1
    width = field.shape[2]
    column = lax.broadcasted_iota(jnp.int32, (1, 1, width, 1), 2)
    outside = ((place == 0) & (column < depth)) | ((place == last) & (column >= width - depth))
    return jnp.where(outside, jnp.zeros_like(field), field)


def rimmed_slope(field):
    return padded_2(field, (("band", 2),), 1)


def forward(current, hidden, memory, obs_weight, obs_target, weights):
    prior_in, prior_out, lstm_weight, lstm_bias, out_weight = weights
    units = out_weight.shape[1]
    state_wide = padded_2(current.astype(jnp.bfloat16), (("band", 2),), 2)
    state_rim = state_wide[:, :, 1:-1]
    pre_prior = conv_three(prior_in, state_wide)
    latent_rim = edge_zeroed(jax.nn.silu(pre_prior).astype(jnp.bfloat16))
    prior_state = conv_three(prior_out, latent_rim)
    cost_slope = obs_weight * current - obs_target + prior_weight * (current - prior_state)
    joined = jnp.concatenate([cost_slope, hidden], axis=1).astype(jnp.bfloat16)
    joined_rim = rimmed_field(joined)
    return lstm_tail(current, memory, state_rim, pre_prior, latent_rim, joined_rim, weights)

def forward_first(current, obs_weight, obs_target, weights):
    prior_in, prior_out, lstm_weight, lstm_bias, out_weight = weights
    units = out_weight.shape[1]
    frames = current.shape[1]
    batch, _, breadth, lat_count = current.shape
    fields = jnp.concatenate([current, obs_weight, obs_target], axis=1)
    wide = padded_2(fields, (("band", 2),), 3)
    current_wide = wide[:, :frames]
    state_wide = current_wide.astype(jnp.bfloat16)
    pre_wide = conv_three(prior_in, state_wide)
    latent_wide = edge_zeroed(jax.nn.silu(pre_wide).astype(jnp.bfloat16), 2)
    prior_state = conv_three(prior_out, latent_wide)
    near = wide[:, :, 2:-2]
    here, weight_near, target_near = near[:, :frames], near[:, frames : 2 * frames], near[:, 2 * frames :]
    cost_slope = weight_near * here - target_near + prior_weight * (here - prior_state)
    hidden_near = jnp.zeros((batch, units, breadth + 2, lat_count), jnp.float32)
    joined_rim = edge_zeroed(jnp.concatenate([cost_slope, hidden_near], axis=1).astype(jnp.bfloat16))
    memory = jnp.zeros((batch, units, breadth, lat_count), jnp.float32)
    state_rim = state_wide[:, :, 2:-2]
    pre_prior = pre_wide[:, :, 1:-1]
    latent_rim = latent_wide[:, :, 1:-1]
    return lstm_tail(current, memory, state_rim, pre_prior, latent_rim, joined_rim, weights)


def lstm_tail(current, memory, state_rim, pre_prior, latent_rim, joined_rim, weights):
    prior_in, prior_out, lstm_weight, lstm_bias, out_weight = weights
    units = out_weight.shape[1]
    gate_all = conv_three(lstm_weight, joined_rim, "io") + lstm_bias[None, :, None, None]
    in_gate = jax.nn.sigmoid(gate_all[:, :units])
    forget_gate = jax.nn.sigmoid(gate_all[:, units : 2 * units])
    out_gate = jax.nn.sigmoid(gate_all[:, 2 * units : 3 * units])
    update = jnp.tanh(gate_all[:, 3 * units :])
    memory_next = forget_gate * memory + in_gate * update
    squashed = jnp.tanh(memory_next)
    hidden_next = out_gate * squashed
    hidden_low = hidden_next.astype(jnp.bfloat16)
    stepped = jnp.einsum(
        "fh,bhwl->bfwl", out_weight, hidden_low, preferred_element_type=jnp.float32
    )
    saved = (
        state_rim,
        pre_prior,
        latent_rim,
        joined_rim,
        in_gate,
        forget_gate,
        out_gate,
        update,
        memory,
        squashed,
        hidden_low,
    )
    return (current - stepped, hidden_next, memory_next, saved)


def backward(slope_state, slope_hidden, slope_memory, saved, obs_weight, weights, leading):
    prior_in, prior_out, lstm_weight, lstm_bias, out_weight = weights
    (
        state_rim,
        pre_prior,
        latent_rim,
        joined_rim,
        in_gate,
        forget_gate,
        out_gate,
        update,
        memory,
        squashed,
        hidden_low,
    ) = saved
    frames = slope_state.shape[1]
    neg_low = (-slope_state).astype(jnp.bfloat16)
    grad_outw = jnp.einsum("bfwl,bhwl->fh", neg_low, hidden_low, preferred_element_type=jnp.float32)
    slope_hid = (
        jnp.einsum("fh,bfwl->bhwl", out_weight, neg_low, preferred_element_type=jnp.float32)
        + slope_hidden
    )
    slope_mem = slope_hid * out_gate * (1.0 - squashed * squashed) + slope_memory
    gate_slope = jnp.concatenate(
        [
            slope_mem * update * in_gate * (1.0 - in_gate),
            slope_mem * memory * forget_gate * (1.0 - forget_gate),
            slope_hid * squashed * out_gate * (1.0 - out_gate),
            slope_mem * in_gate * (1.0 - update * update),
        ],
        axis=1,
    )
    grad_bias = jnp.sum(gate_slope, axis=(0, 2, 3))
    gate_low = gate_slope.astype(jnp.bfloat16)
    grad_lstm = kernel_slope(gate_low, joined_rim, "io")
    back_kernel = lstm_weight[::-1]
    if leading:
        back_kernel = back_kernel[:, :frames]
    gate_rimmed = padded_2(gate_low, (("band", 2),), 1)
    joined_slope = conv_three(back_kernel, gate_rimmed)
    cost_part = joined_slope[:, :frames]
    hidden_back = None if leading else joined_slope[:, frames:]
    slope_prev = slope_state + (obs_weight + prior_weight) * cost_part
    prior_low = (-prior_weight * cost_part).astype(jnp.bfloat16)
    grad_pout = kernel_slope(prior_low, latent_rim)
    latent_slope = conv_three(flipped(prior_out), padded_2(prior_low, (("band", 2),), 2))
    sigma = jax.nn.sigmoid(pre_prior)
    pre_rim = (latent_slope * (sigma + pre_prior * sigma * (1.0 - sigma))).astype(jnp.bfloat16)
    pre_rim = edge_zeroed(pre_rim)
    grad_pin = kernel_slope(pre_rim[:, :, 1:-1], state_rim)
    slope_prev = slope_prev + conv_three(flipped(prior_in), pre_rim)
    memory_back = slope_mem * forget_gate
    return (
        slope_prev,
        hidden_back,
        memory_back,
        (grad_pin, grad_pout, grad_lstm, grad_bias, grad_outw),
    )


def body(
    first_guess,
    observed_height,
    swath_cells,
    drift_value,
    drift_cell,
    prior_in,
    prior_out,
    lstm_weight,
    lstm_bias,
    out_weight,
    final_slope,
):
    batch, frames, breadth, lat_count = first_guess.shape
    block = breadth * lat_count
    spots = jnp.arange(block, dtype=jnp.int32)
    hits = swath_cells[:, :, 0, :, None] == spots
    mask = jnp.any(hits, axis=2).astype(jnp.float32).reshape(batch, frames, breadth, lat_count)
    packed = jnp.stack([drift_value, drift_cell.astype(jnp.float32)])
    arrived = lax.all_to_all(packed, "band", split_axis=3, concat_axis=2, tiled=True)
    arrived_value = arrived[0].reshape(batch, -1)
    arrived_cell = arrived[1].astype(jnp.int32).reshape(batch, -1)
    places = jnp.arange(frames * block, dtype=jnp.int32).reshape(frames, breadth, lat_count)
    landed = arrived_cell[:, :, None, None, None] == places
    drift_count = jnp.sum(landed.astype(jnp.float32), axis=1)
    drift_total = jnp.sum(jnp.where(landed, arrived_value[:, :, None, None, None], 0.0), axis=1)
    obs_weight = mask + drift_count
    obs_target = mask * observed_height + drift_total
    weights = (prior_in, prior_out, lstm_weight, lstm_bias, out_weight)
    units = out_weight.shape[1]
    blank = jnp.zeros((batch, units, breadth, lat_count), jnp.float32)
    state_one, hid_one, mem_one, saved_one = forward_first(first_guess, obs_weight, obs_target, weights)
    state_two, hid_two, mem_two, saved_two = forward(
        state_one, hid_one, mem_one, obs_weight, obs_target, weights
    )
    slope_mid, hidden_back, memory_back, grads_two = backward(
        final_slope, blank, blank, saved_two, obs_weight, weights, False
    )
    slope_start, unused_hid, unused_mem, grads_one = backward(
        slope_mid, hidden_back, memory_back, saved_one, obs_weight, weights, True
    )
    summed = jax.tree.map(jnp.add, grads_one, grads_two)
    cells_all = batch * lax.axis_size("win") * breadth * lax.axis_size("band") * lat_count
    scale = 1.0 / jnp.sqrt(jnp.float32(cells_all))
    grad_pin, grad_pout, grad_lstm, grad_bias, grad_outw = summed
    taps, ins, outs = grad_lstm.shape
    rows = jnp.pad(grad_lstm, ((0, 0), (0, (-ins) % 8), (0, 0))).reshape(-1, outs)
    lstm_total = summed_everywhere(rows, "band", "win", jnp.bfloat16)
    lstm_total = lstm_total.reshape(taps, -1, outs)[:, :ins]
    small = [grad_pin, grad_pout, grad_bias, grad_outw]
    flat = jnp.concatenate([member.reshape(-1) for member in small])
    flat = summed_everywhere(flat, "band", "win")
    totals = []
    offset = 0
    for member in small:
        length = member.size
        totals.append(flat[offset : offset + length].reshape(member.shape))
        offset = offset + length
    totals = [totals[0], totals[1], lstm_total, totals[2], totals[3]]
    return (
        slope_start,
        totals[0] * scale,
        totals[1] * scale,
        totals[2] * scale,
        totals[3] * scale,
        totals[4] * scale,
    )


def summed_everywhere(flat, outer, inner, gathered=None):
    bands, wins = lax.axis_size(outer), lax.axis_size(inner)
    count = bands * wins
    if count & (count - 1):
        return lax.psum(flat, (outer, inner))
    axes = (outer, inner)
    inner_bits = wins.bit_length() - 1
    levels = (count.bit_length() - 1)
    order = ([inner_bits] if inner_bits < levels else []) + list(range(inner_bits)) + list(range(inner_bits + 1, levels))
    me = lax.axis_index(axes)
    extent = flat.shape[0]
    cur = jnp.pad(flat, [(0, (-extent) % count)] + [(0, 0)] * (flat.ndim - 1))
    for level in order:
        mask = 1 << level
        half = cur.shape[0] // 2
        high = (me & mask) != 0
        low_part, high_part = cur[:half], cur[half:]
        keep = jnp.where(high, high_part, low_part)
        send = jnp.where(high, low_part, high_part)
        cur = keep + lax.ppermute(send, axes, [(i, i ^ mask) for i in range(count)])
    total_type = cur.dtype
    if gathered is not None:
        cur = cur.astype(gathered)
    for level in reversed(order):
        mask = 1 << level
        high = (me & mask) != 0
        other = lax.ppermute(cur, axes, [(i, i ^ mask) for i in range(count)])
        cur = jnp.where(high, jnp.concatenate([other, cur]), jnp.concatenate([cur, other]))
    return cur[:extent].astype(total_type)


def solution(mesh):
    return jax.shard_map(
        body,
        mesh=mesh,
        in_specs=(
            P("win", None, "band", None),
            P("win", None, "band", None),
            P("win", None, "band", None),
            P("win", "band", None, None),
            P("win", "band", None, None),
            P(),
            P(),
            P(),
            P(),
            P(),
            P("win", None, "band", None),
        ),
        out_specs=(P("win", None, "band", None), P(), P(), P(), P(), P()),
        check_vma=False,
    )
```

```python
import jax
import jax.numpy as jnp
from jax import lax
from jax.sharding import PartitionSpec as P

prior_weight = 1.0


def padded_2(array, sides, width):
    for axis, dim in sides:
        size, length = (lax.axis_size(axis), array.shape[dim])
        up = [(i, (i + 1) % size) for i in range(size - 1)]
        down = [(j, i) for i, j in up]
        last = lax.slice_in_dim(array, length - width, length, axis=dim)
        first = lax.slice_in_dim(array, 0, width, axis=dim)
        before = lax.ppermute(last, axis, up)
        after = lax.ppermute(first, axis, down)
        array = jnp.concatenate([before, array, after], axis=dim)
    return array


def conv_three(kernel, padded, form="oi"):
    breadth = padded.shape[2] - 2
    lat_count = padded.shape[3]
    framed = jnp.pad(padded, ((0, 0), (0, 0), (0, 0), (1, 1)))
    summed = None
    for lon_off in range(3):
        for lat_off in range(3):
            window = framed[:, :, lon_off : lon_off + breadth, lat_off : lat_off + lat_count]
            contrib = jnp.einsum(
                form + ",biwl->bowl",
                kernel[3 * lon_off + lat_off],
                window,
                preferred_element_type=jnp.float32,
            )
            summed = contrib if summed is None else summed + contrib
    return summed


def kernel_slope(cotangent, padded, form="oi"):
    breadth = cotangent.shape[2]
    lat_count = cotangent.shape[3]
    framed = jnp.pad(padded, ((0, 0), (0, 0), (0, 0), (1, 1)))
    pieces = []
    for lon_off in range(3):
        for lat_off in range(3):
            window = framed[:, :, lon_off : lon_off + breadth, lat_off : lat_off + lat_count]
            pieces.append(
                jnp.einsum(
                    "bowl,biwl->" + form, cotangent, window, preferred_element_type=jnp.float32
                )
            )
    return jnp.stack(pieces)


def flipped(kernel):
    return jnp.transpose(kernel[::-1], (0, 2, 1))


def rimmed_field(field):
    return padded_2(field, (("band", 2),), 1)


def edge_zeroed(field, depth=1):
    place = lax.axis_index("band")
    last = lax.axis_size("band") - 1
    width = field.shape[2]
    column = lax.broadcasted_iota(jnp.int32, (1, 1, width, 1), 2)
    outside = ((place == 0) & (column < depth)) | ((place == last) & (column >= width - depth))
    return jnp.where(outside, jnp.zeros_like(field), field)


def rimmed_slope(field):
    return padded_2(field, (("band", 2),), 1)


def forward(current, hidden, memory, obs_weight, obs_target, weights):
    prior_in, prior_out, lstm_weight, lstm_bias, out_weight = weights
    units = out_weight.shape[1]
    state_wide = padded_2(current.astype(jnp.bfloat16), (("band", 2),), 2)
    state_rim = state_wide[:, :, 1:-1]
    pre_prior = conv_three(prior_in, state_wide)
    latent_rim = edge_zeroed(jax.nn.silu(pre_prior).astype(jnp.bfloat16))
    prior_state = conv_three(prior_out, latent_rim)
    cost_slope = obs_weight * current - obs_target + prior_weight * (current - prior_state)
    joined = jnp.concatenate([cost_slope, hidden], axis=1).astype(jnp.bfloat16)
    joined_rim = rimmed_field(joined)
    return lstm_tail(current, memory, state_rim, pre_prior, latent_rim, joined_rim, weights)

def forward_first(current, obs_weight, obs_target, weights):
    prior_in, prior_out, lstm_weight, lstm_bias, out_weight = weights
    units = out_weight.shape[1]
    frames = current.shape[1]
    batch, _, breadth, lat_count = current.shape
    fields = jnp.concatenate([current, obs_weight, obs_target], axis=1)
    wide = padded_2(fields, (("band", 2),), 3)
    current_wide = wide[:, :frames]
    state_wide = current_wide.astype(jnp.bfloat16)
    pre_wide = conv_three(prior_in, state_wide)
    latent_wide = edge_zeroed(jax.nn.silu(pre_wide).astype(jnp.bfloat16), 2)
    prior_state = conv_three(prior_out, latent_wide)
    near = wide[:, :, 2:-2]
    here, weight_near, target_near = near[:, :frames], near[:, frames : 2 * frames], near[:, 2 * frames :]
    cost_slope = weight_near * here - target_near + prior_weight * (here - prior_state)
    hidden_near = jnp.zeros((batch, units, breadth + 2, lat_count), jnp.float32)
    joined_rim = edge_zeroed(jnp.concatenate([cost_slope, hidden_near], axis=1).astype(jnp.bfloat16))
    memory = jnp.zeros((batch, units, breadth, lat_count), jnp.float32)
    state_rim = state_wide[:, :, 2:-2]
    pre_prior = pre_wide[:, :, 1:-1]
    latent_rim = latent_wide[:, :, 1:-1]
    return lstm_tail(current, memory, state_rim, pre_prior, latent_rim, joined_rim, weights)


def lstm_tail(current, memory, state_rim, pre_prior, latent_rim, joined_rim, weights):
    prior_in, prior_out, lstm_weight, lstm_bias, out_weight = weights
    units = out_weight.shape[1]
    gate_all = conv_three(lstm_weight, joined_rim, "io") + lstm_bias[None, :, None, None]
    in_gate = jax.nn.sigmoid(gate_all[:, :units])
    forget_gate = jax.nn.sigmoid(gate_all[:, units : 2 * units])
    out_gate = jax.nn.sigmoid(gate_all[:, 2 * units : 3 * units])
    update = jnp.tanh(gate_all[:, 3 * units :])
    memory_next = forget_gate * memory + in_gate * update
    squashed = jnp.tanh(memory_next)
    hidden_next = out_gate * squashed
    hidden_low = hidden_next.astype(jnp.bfloat16)
    stepped = jnp.einsum(
        "fh,bhwl->bfwl", out_weight, hidden_low, preferred_element_type=jnp.float32
    )
    saved = (
        state_rim,
        pre_prior,
        latent_rim,
        joined_rim,
        in_gate,
        forget_gate,
        out_gate,
        update,
        memory,
        squashed,
        hidden_low,
    )
    return (current - stepped, hidden_next, memory_next, saved)


def backward(slope_state, slope_hidden, slope_memory, saved, obs_weight, weights, leading):
    prior_in, prior_out, lstm_weight, lstm_bias, out_weight = weights
    (
        state_rim,
        pre_prior,
        latent_rim,
        joined_rim,
        in_gate,
        forget_gate,
        out_gate,
        update,
        memory,
        squashed,
        hidden_low,
    ) = saved
    frames = slope_state.shape[1]
    neg_low = (-slope_state).astype(jnp.bfloat16)
    grad_outw = jnp.einsum("bfwl,bhwl->fh", neg_low, hidden_low, preferred_element_type=jnp.float32)
    slope_hid = (
        jnp.einsum("fh,bfwl->bhwl", out_weight, neg_low, preferred_element_type=jnp.float32)
        + slope_hidden
    )
    slope_mem = slope_hid * out_gate * (1.0 - squashed * squashed) + slope_memory
    gate_slope = jnp.concatenate(
        [
            slope_mem * update * in_gate * (1.0 - in_gate),
            slope_mem * memory * forget_gate * (1.0 - forget_gate),
            slope_hid * squashed * out_gate * (1.0 - out_gate),
            slope_mem * in_gate * (1.0 - update * update),
        ],
        axis=1,
    )
    grad_bias = jnp.sum(gate_slope, axis=(0, 2, 3))
    gate_low = gate_slope.astype(jnp.bfloat16)
    grad_lstm = kernel_slope(gate_low, joined_rim, "io")
    back_kernel = lstm_weight[::-1]
    if leading:
        back_kernel = back_kernel[:, :frames]
    gate_rimmed = padded_2(gate_low, (("band", 2),), 1)
    joined_slope = conv_three(back_kernel, gate_rimmed)
    cost_part = joined_slope[:, :frames]
    hidden_back = None if leading else joined_slope[:, frames:]
    slope_prev = slope_state + (obs_weight + prior_weight) * cost_part
    prior_low = (-prior_weight * cost_part).astype(jnp.bfloat16)
    grad_pout = kernel_slope(prior_low, latent_rim)
    latent_slope = conv_three(flipped(prior_out), padded_2(prior_low, (("band", 2),), 2))
    sigma = jax.nn.sigmoid(pre_prior)
    pre_rim = (latent_slope * (sigma + pre_prior * sigma * (1.0 - sigma))).astype(jnp.bfloat16)
    pre_rim = edge_zeroed(pre_rim)
    grad_pin = kernel_slope(pre_rim[:, :, 1:-1], state_rim)
    slope_prev = slope_prev + conv_three(flipped(prior_in), pre_rim)
    memory_back = slope_mem * forget_gate
    return (
        slope_prev,
        hidden_back,
        memory_back,
        (grad_pin, grad_pout, grad_lstm, grad_bias, grad_outw),
    )


def body(
    first_guess,
    observed_height,
    swath_cells,
    drift_value,
    drift_cell,
    prior_in,
    prior_out,
    lstm_weight,
    lstm_bias,
    out_weight,
    final_slope,
):
    batch, frames, breadth, lat_count = first_guess.shape
    block = breadth * lat_count
    spots = jnp.arange(block, dtype=jnp.int32)
    hits = swath_cells[:, :, 0, :, None] == spots
    mask = jnp.any(hits, axis=2).astype(jnp.float32).reshape(batch, frames, breadth, lat_count)
    packed = jnp.stack([drift_value, drift_cell.astype(jnp.float32)])
    arrived = lax.all_to_all(packed, "band", split_axis=3, concat_axis=2, tiled=True)
    arrived_value = arrived[0].reshape(batch, -1)
    arrived_cell = arrived[1].astype(jnp.int32).reshape(batch, -1)
    places = jnp.arange(frames * block, dtype=jnp.int32).reshape(frames, breadth, lat_count)
    landed = arrived_cell[:, :, None, None, None] == places
    drift_count = jnp.sum(landed.astype(jnp.float32), axis=1)
    drift_total = jnp.sum(jnp.where(landed, arrived_value[:, :, None, None, None], 0.0), axis=1)
    obs_weight = mask + drift_count
    obs_target = mask * observed_height + drift_total
    weights = (prior_in, prior_out, lstm_weight, lstm_bias, out_weight)
    units = out_weight.shape[1]
    blank = jnp.zeros((batch, units, breadth, lat_count), jnp.float32)
    state_one, hid_one, mem_one, saved_one = forward_first(first_guess, obs_weight, obs_target, weights)
    state_two, hid_two, mem_two, saved_two = forward(
        state_one, hid_one, mem_one, obs_weight, obs_target, weights
    )
    slope_mid, hidden_back, memory_back, grads_two = backward(
        final_slope, blank, blank, saved_two, obs_weight, weights, False
    )
    slope_start, unused_hid, unused_mem, grads_one = backward(
        slope_mid, hidden_back, memory_back, saved_one, obs_weight, weights, True
    )
    summed = jax.tree.map(jnp.add, grads_one, grads_two)
    cells_all = batch * lax.axis_size("win") * breadth * lax.axis_size("band") * lat_count
    scale = 1.0 / jnp.sqrt(jnp.float32(cells_all))
    grad_pin, grad_pout, grad_lstm, grad_bias, grad_outw = summed
    taps, ins, outs = grad_lstm.shape
    rows = jnp.pad(grad_lstm, ((0, 0), (0, (-ins) % 8), (0, 0))).reshape(-1, outs)
    lstm_total = summed_everywhere(rows, "band", "win", jnp.bfloat16)
    lstm_total = lstm_total.reshape(taps, -1, outs)[:, :ins]
    small = [grad_pin, grad_pout, grad_bias, grad_outw]
    flat = jnp.concatenate([member.reshape(-1) for member in small])
    flat = summed_butterfly(flat, "band", "win")
    totals = []
    offset = 0
    for member in small:
        length = member.size
        totals.append(flat[offset : offset + length].reshape(member.shape))
        offset = offset + length
    totals = [totals[0], totals[1], lstm_total, totals[2], totals[3]]
    return (
        slope_start,
        totals[0] * scale,
        totals[1] * scale,
        totals[2] * scale,
        totals[3] * scale,
        totals[4] * scale,
    )


def summed_everywhere(flat, outer, inner, gathered=None):
    bands, wins = lax.axis_size(outer), lax.axis_size(inner)
    count = bands * wins
    if count & (count - 1):
        return lax.psum(flat, (outer, inner))
    axes = (outer, inner)
    inner_bits = wins.bit_length() - 1
    levels = (count.bit_length() - 1)
    order = ([inner_bits] if inner_bits < levels else []) + list(range(inner_bits)) + list(range(inner_bits + 1, levels))
    me = lax.axis_index(axes)
    extent = flat.shape[0]
    cur = jnp.pad(flat, [(0, (-extent) % count)] + [(0, 0)] * (flat.ndim - 1))
    for level in order:
        mask = 1 << level
        half = cur.shape[0] // 2
        high = (me & mask) != 0
        low_part, high_part = cur[:half], cur[half:]
        keep = jnp.where(high, high_part, low_part)
        send = jnp.where(high, low_part, high_part)
        cur = keep + lax.ppermute(send, axes, [(i, i ^ mask) for i in range(count)])
    total_type = cur.dtype
    if gathered is not None:
        cur = cur.astype(gathered)
    for level in reversed(order):
        mask = 1 << level
        high = (me & mask) != 0
        other = lax.ppermute(cur, axes, [(i, i ^ mask) for i in range(count)])
        cur = jnp.where(high, jnp.concatenate([other, cur]), jnp.concatenate([cur, other]))
    return cur[:extent].astype(total_type)


def summed_butterfly(flat, outer, inner):
    bands, wins = lax.axis_size(outer), lax.axis_size(inner)
    count = bands * wins
    if count & (count - 1):
        return lax.psum(flat, (outer, inner))
    axes = (outer, inner)
    inner_bits = wins.bit_length() - 1
    levels = count.bit_length() - 1
    order = ([inner_bits] if inner_bits < levels else []) + list(range(inner_bits)) + list(range(inner_bits + 1, levels))
    for level in order:
        mask = 1 << level
        flat = flat + lax.ppermute(flat, axes, [(i, i ^ mask) for i in range(count)])
    return flat


def solution(mesh):
    return jax.shard_map(
        body,
        mesh=mesh,
        in_specs=(
            P("win", None, "band", None),
            P("win", None, "band", None),
            P("win", None, "band", None),
            P("win", "band", None, None),
            P("win", "band", None, None),
            P(),
            P(),
            P(),
            P(),
            P(),
            P("win", None, "band", None),
        ),
        out_specs=(P("win", None, "band", None), P(), P(), P(), P(), P()),
        check_vma=False,
    )
```

```python
import jax
import jax.numpy as jnp
from jax import lax
from jax.sharding import PartitionSpec as P

prior_weight = 1.0


def padded_2(array, sides, width):
    for axis, dim in sides:
        size, length = (lax.axis_size(axis), array.shape[dim])
        up = [(i, (i + 1) % size) for i in range(size - 1)]
        down = [(j, i) for i, j in up]
        last = lax.slice_in_dim(array, length - width, length, axis=dim)
        first = lax.slice_in_dim(array, 0, width, axis=dim)
        before = lax.ppermute(last, axis, up)
        after = lax.ppermute(first, axis, down)
        array = jnp.concatenate([before, array, after], axis=dim)
    return array


def conv_three(kernel, padded, form="oi"):
    breadth = padded.shape[2] - 2
    lat_count = padded.shape[3]
    framed = jnp.pad(padded, ((0, 0), (0, 0), (0, 0), (1, 1)))
    summed = None
    for lon_off in range(3):
        for lat_off in range(3):
            window = framed[:, :, lon_off : lon_off + breadth, lat_off : lat_off + lat_count]
            contrib = jnp.einsum(
                form + ",biwl->bowl",
                kernel[3 * lon_off + lat_off],
                window,
                preferred_element_type=jnp.float32,
            )
            summed = contrib if summed is None else summed + contrib
    return summed


def kernel_slope(cotangent, padded, form="oi"):
    breadth = cotangent.shape[2]
    lat_count = cotangent.shape[3]
    framed = jnp.pad(padded, ((0, 0), (0, 0), (0, 0), (1, 1)))
    pieces = []
    for lon_off in range(3):
        for lat_off in range(3):
            window = framed[:, :, lon_off : lon_off + breadth, lat_off : lat_off + lat_count]
            pieces.append(
                jnp.einsum(
                    "bowl,biwl->" + form, cotangent, window, preferred_element_type=jnp.float32
                )
            )
    return jnp.stack(pieces)


def flipped(kernel):
    return jnp.transpose(kernel[::-1], (0, 2, 1))


def rimmed_field(field):
    return padded_2(field, (("band", 2),), 1)


def edge_zeroed(field, depth=1):
    place = lax.axis_index("band")
    last = lax.axis_size("band") - 1
    width = field.shape[2]
    column = lax.broadcasted_iota(jnp.int32, (1, 1, width, 1), 2)
    outside = ((place == 0) & (column < depth)) | ((place == last) & (column >= width - depth))
    return jnp.where(outside, jnp.zeros_like(field), field)


def rimmed_slope(field):
    return padded_2(field, (("band", 2),), 1)


def forward(current, hidden, memory, obs_weight, obs_target, weights):
    prior_in, prior_out, lstm_weight, lstm_bias, out_weight = weights
    units = out_weight.shape[1]
    state_wide = padded_2(current.astype(jnp.bfloat16), (("band", 2),), 2)
    state_rim = state_wide[:, :, 1:-1]
    pre_prior = conv_three(prior_in, state_wide)
    latent_rim = edge_zeroed(jax.nn.silu(pre_prior).astype(jnp.bfloat16))
    prior_state = conv_three(prior_out, latent_rim)
    cost_slope = obs_weight * current - obs_target + prior_weight * (current - prior_state)
    joined = jnp.concatenate([cost_slope, hidden], axis=1).astype(jnp.bfloat16)
    joined_rim = rimmed_field(joined)
    return lstm_tail(current, memory, state_rim, pre_prior, latent_rim, joined_rim, weights)

def forward_first(current, obs_weight, obs_target, weights):
    prior_in, prior_out, lstm_weight, lstm_bias, out_weight = weights
    units = out_weight.shape[1]
    frames = current.shape[1]
    batch, _, breadth, lat_count = current.shape
    fields = jnp.concatenate([current, obs_weight, obs_target], axis=1)
    wide = padded_2(fields, (("band", 2),), 3)
    current_wide = wide[:, :frames]
    state_wide = current_wide.astype(jnp.bfloat16)
    pre_wide = conv_three(prior_in, state_wide)
    latent_wide = edge_zeroed(jax.nn.silu(pre_wide).astype(jnp.bfloat16), 2)
    prior_state = conv_three(prior_out, latent_wide)
    near = wide[:, :, 2:-2]
    here, weight_near, target_near = near[:, :frames], near[:, frames : 2 * frames], near[:, 2 * frames :]
    cost_slope = weight_near * here - target_near + prior_weight * (here - prior_state)
    hidden_near = jnp.zeros((batch, units, breadth + 2, lat_count), jnp.float32)
    joined_rim = edge_zeroed(jnp.concatenate([cost_slope, hidden_near], axis=1).astype(jnp.bfloat16))
    memory = jnp.zeros((batch, units, breadth, lat_count), jnp.float32)
    state_rim = state_wide[:, :, 2:-2]
    pre_prior = pre_wide[:, :, 1:-1]
    latent_rim = latent_wide[:, :, 1:-1]
    return lstm_tail(current, memory, state_rim, pre_prior, latent_rim, joined_rim, weights)


def lstm_tail(current, memory, state_rim, pre_prior, latent_rim, joined_rim, weights):
    prior_in, prior_out, lstm_weight, lstm_bias, out_weight = weights
    units = out_weight.shape[1]
    gate_all = conv_three(lstm_weight, joined_rim, "io") + lstm_bias[None, :, None, None]
    in_gate = jax.nn.sigmoid(gate_all[:, :units])
    forget_gate = jax.nn.sigmoid(gate_all[:, units : 2 * units])
    out_gate = jax.nn.sigmoid(gate_all[:, 2 * units : 3 * units])
    update = jnp.tanh(gate_all[:, 3 * units :])
    memory_next = forget_gate * memory + in_gate * update
    squashed = jnp.tanh(memory_next)
    hidden_next = out_gate * squashed
    hidden_low = hidden_next.astype(jnp.bfloat16)
    stepped = jnp.einsum(
        "fh,bhwl->bfwl", out_weight, hidden_low, preferred_element_type=jnp.float32
    )
    saved = (
        state_rim,
        pre_prior,
        latent_rim,
        joined_rim,
        in_gate,
        forget_gate,
        out_gate,
        update,
        memory,
        squashed,
        hidden_low,
    )
    return (current - stepped, hidden_next, memory_next, saved)


def backward(slope_state, slope_hidden, slope_memory, saved, obs_weight, weights, leading):
    prior_in, prior_out, lstm_weight, lstm_bias, out_weight = weights
    (
        state_rim,
        pre_prior,
        latent_rim,
        joined_rim,
        in_gate,
        forget_gate,
        out_gate,
        update,
        memory,
        squashed,
        hidden_low,
    ) = saved
    frames = slope_state.shape[1]
    neg_low = (-slope_state).astype(jnp.bfloat16)
    grad_outw = jnp.einsum("bfwl,bhwl->fh", neg_low, hidden_low, preferred_element_type=jnp.float32)
    slope_hid = (
        jnp.einsum("fh,bfwl->bhwl", out_weight, neg_low, preferred_element_type=jnp.float32)
        + slope_hidden
    )
    slope_mem = slope_hid * out_gate * (1.0 - squashed * squashed) + slope_memory
    gate_slope = jnp.concatenate(
        [
            slope_mem * update * in_gate * (1.0 - in_gate),
            slope_mem * memory * forget_gate * (1.0 - forget_gate),
            slope_hid * squashed * out_gate * (1.0 - out_gate),
            slope_mem * in_gate * (1.0 - update * update),
        ],
        axis=1,
    )
    grad_bias = jnp.sum(gate_slope, axis=(0, 2, 3))
    gate_low = gate_slope.astype(jnp.bfloat16)
    grad_lstm = kernel_slope(gate_low, joined_rim, "io")
    back_kernel = lstm_weight[::-1]
    if leading:
        back_kernel = back_kernel[:, :frames]
    gate_rimmed = padded_2(gate_low, (("band", 2),), 1)
    joined_slope = conv_three(back_kernel, gate_rimmed)
    cost_part = joined_slope[:, :frames]
    hidden_back = None if leading else joined_slope[:, frames:]
    slope_prev = slope_state + (obs_weight + prior_weight) * cost_part
    prior_low = (-prior_weight * cost_part).astype(jnp.bfloat16)
    grad_pout = kernel_slope(prior_low, latent_rim)
    latent_slope = conv_three(flipped(prior_out), padded_2(prior_low, (("band", 2),), 2))
    sigma = jax.nn.sigmoid(pre_prior)
    pre_rim = (latent_slope * (sigma + pre_prior * sigma * (1.0 - sigma))).astype(jnp.bfloat16)
    pre_rim = edge_zeroed(pre_rim)
    grad_pin = kernel_slope(pre_rim[:, :, 1:-1], state_rim)
    slope_prev = slope_prev + conv_three(flipped(prior_in), pre_rim)
    memory_back = slope_mem * forget_gate
    return (
        slope_prev,
        hidden_back,
        memory_back,
        (grad_pin, grad_pout, grad_lstm, grad_bias, grad_outw),
    )


def body(
    first_guess,
    observed_height,
    swath_cells,
    drift_value,
    drift_cell,
    prior_in,
    prior_out,
    lstm_weight,
    lstm_bias,
    out_weight,
    final_slope,
):
    batch, frames, breadth, lat_count = first_guess.shape
    block = breadth * lat_count
    spots = jnp.arange(block, dtype=jnp.int32)
    hits = swath_cells[:, :, 0, :, None] == spots
    mask = jnp.any(hits, axis=2).astype(jnp.float32).reshape(batch, frames, breadth, lat_count)
    packed = jnp.stack([drift_value, drift_cell.astype(jnp.float32)])
    arrived = lax.all_to_all(packed, "band", split_axis=3, concat_axis=2, tiled=True)
    arrived_value = arrived[0].reshape(batch, -1)
    arrived_cell = arrived[1].astype(jnp.int32).reshape(batch, -1)
    places = jnp.arange(frames * block, dtype=jnp.int32).reshape(frames, breadth, lat_count)
    landed = arrived_cell[:, :, None, None, None] == places
    drift_count = jnp.sum(landed.astype(jnp.float32), axis=1)
    drift_total = jnp.sum(jnp.where(landed, arrived_value[:, :, None, None, None], 0.0), axis=1)
    obs_weight = mask + drift_count
    obs_target = mask * observed_height + drift_total
    weights = (prior_in, prior_out, lstm_weight, lstm_bias, out_weight)
    units = out_weight.shape[1]
    blank = jnp.zeros((batch, units, breadth, lat_count), jnp.float32)
    state_one, hid_one, mem_one, saved_one = forward_first(first_guess, obs_weight, obs_target, weights)
    state_two, hid_two, mem_two, saved_two = forward(
        state_one, hid_one, mem_one, obs_weight, obs_target, weights
    )
    slope_mid, hidden_back, memory_back, grads_two = backward(
        final_slope, blank, blank, saved_two, obs_weight, weights, False
    )
    slope_start, unused_hid, unused_mem, grads_one = backward(
        slope_mid, hidden_back, memory_back, saved_one, obs_weight, weights, True
    )
    summed = jax.tree.map(jnp.add, grads_one, grads_two)
    cells_all = batch * lax.axis_size("win") * breadth * lax.axis_size("band") * lat_count
    scale = 1.0 / jnp.sqrt(jnp.float32(cells_all))
    grad_pin, grad_pout, grad_lstm, grad_bias, grad_outw = summed
    taps, ins, outs = grad_lstm.shape
    rows = jnp.pad(grad_lstm, ((0, 0), (0, (-ins) % 8), (0, 0))).reshape(-1, outs)
    lstm_total = summed_everywhere(rows, "band", "win", jnp.bfloat16)
    lstm_total = lstm_total.reshape(taps, -1, outs)[:, :ins]
    small = [grad_pin, grad_pout, grad_bias, grad_outw]
    flat = jnp.concatenate([member.reshape(-1) for member in small])
    flat = summed_butterfly(flat, "band", "win")
    totals = []
    offset = 0
    for member in small:
        length = member.size
        totals.append(flat[offset : offset + length].reshape(member.shape))
        offset = offset + length
    totals = [totals[0], totals[1], lstm_total, totals[2], totals[3]]
    return (
        slope_start,
        totals[0] * scale,
        totals[1] * scale,
        totals[2] * scale,
        totals[3] * scale,
        totals[4] * scale,
    )


def summed_everywhere(flat, outer, inner, gathered=None):
    bands, wins = lax.axis_size(outer), lax.axis_size(inner)
    count = bands * wins
    if count & (count - 1):
        return lax.psum(flat, (outer, inner))
    axes = (outer, inner)
    inner_bits = wins.bit_length() - 1
    levels = (count.bit_length() - 1)
    order = ([inner_bits] if inner_bits < levels else []) + list(range(inner_bits)) + list(range(inner_bits + 1, levels))
    me = lax.axis_index(axes)
    extent = flat.shape[0]
    cur = jnp.pad(flat, [(0, (-extent) % count)] + [(0, 0)] * (flat.ndim - 1))
    split = order[:-2] if len(order) > 2 else order
    for level in split:
        mask = 1 << level
        half = cur.shape[0] // 2
        high = (me & mask) != 0
        low_part, high_part = cur[:half], cur[half:]
        keep = jnp.where(high, high_part, low_part)
        send = jnp.where(high, low_part, high_part)
        cur = keep + lax.ppermute(send, axes, [(i, i ^ mask) for i in range(count)])
    for level in order[len(split):]:
        mask = 1 << level
        cur = cur + lax.ppermute(cur, axes, [(i, i ^ mask) for i in range(count)])
    total_type = cur.dtype
    if gathered is not None:
        cur = cur.astype(gathered)
    for level in reversed(split):
        mask = 1 << level
        high = (me & mask) != 0
        other = lax.ppermute(cur, axes, [(i, i ^ mask) for i in range(count)])
        cur = jnp.where(high, jnp.concatenate([other, cur]), jnp.concatenate([cur, other]))
    return cur[:extent].astype(total_type)


def summed_butterfly(flat, outer, inner):
    bands, wins = lax.axis_size(outer), lax.axis_size(inner)
    count = bands * wins
    if count & (count - 1):
        return lax.psum(flat, (outer, inner))
    axes = (outer, inner)
    inner_bits = wins.bit_length() - 1
    levels = count.bit_length() - 1
    order = ([inner_bits] if inner_bits < levels else []) + list(range(inner_bits)) + list(range(inner_bits + 1, levels))
    for level in order:
        mask = 1 << level
        flat = flat + lax.ppermute(flat, axes, [(i, i ^ mask) for i in range(count)])
    return flat


def solution(mesh):
    return jax.shard_map(
        body,
        mesh=mesh,
        in_specs=(
            P("win", None, "band", None),
            P("win", None, "band", None),
            P("win", None, "band", None),
            P("win", "band", None, None),
            P("win", "band", None, None),
            P(),
            P(),
            P(),
            P(),
            P(),
            P("win", None, "band", None),
        ),
        out_specs=(P("win", None, "band", None), P(), P(), P(), P(), P()),
        check_vma=False,
    )
```

```python
import jax
import jax.numpy as jnp
from jax import lax
from jax.sharding import PartitionSpec as P

prior_weight = 1.0


def padded_2(array, sides, width):
    for axis, dim in sides:
        size, length = (lax.axis_size(axis), array.shape[dim])
        up = [(i, (i + 1) % size) for i in range(size - 1)]
        down = [(j, i) for i, j in up]
        last = lax.slice_in_dim(array, length - width, length, axis=dim)
        first = lax.slice_in_dim(array, 0, width, axis=dim)
        before = lax.ppermute(last, axis, up)
        after = lax.ppermute(first, axis, down)
        array = jnp.concatenate([before, array, after], axis=dim)
    return array


def conv_three(kernel, padded, form="oi"):
    breadth = padded.shape[2] - 2
    lat_count = padded.shape[3]
    framed = jnp.pad(padded, ((0, 0), (0, 0), (0, 0), (1, 1)))
    summed = None
    for lon_off in range(3):
        for lat_off in range(3):
            window = framed[:, :, lon_off : lon_off + breadth, lat_off : lat_off + lat_count]
            contrib = jnp.einsum(
                form + ",biwl->bowl",
                kernel[3 * lon_off + lat_off],
                window,
                preferred_element_type=jnp.float32,
            )
            summed = contrib if summed is None else summed + contrib
    return summed


def kernel_slope(cotangent, padded, form="oi"):
    breadth = cotangent.shape[2]
    lat_count = cotangent.shape[3]
    framed = jnp.pad(padded, ((0, 0), (0, 0), (0, 0), (1, 1)))
    pieces = []
    for lon_off in range(3):
        for lat_off in range(3):
            window = framed[:, :, lon_off : lon_off + breadth, lat_off : lat_off + lat_count]
            pieces.append(
                jnp.einsum(
                    "bowl,biwl->" + form, cotangent, window, preferred_element_type=jnp.float32
                )
            )
    return jnp.stack(pieces)


def flipped(kernel):
    return jnp.transpose(kernel[::-1], (0, 2, 1))


def rimmed_field(field):
    return padded_2(field, (("band", 2),), 1)


def edge_zeroed(field, depth=1):
    place = lax.axis_index("band")
    last = lax.axis_size("band") - 1
    width = field.shape[2]
    column = lax.broadcasted_iota(jnp.int32, (1, 1, width, 1), 2)
    outside = ((place == 0) & (column < depth)) | ((place == last) & (column >= width - depth))
    return jnp.where(outside, jnp.zeros_like(field), field)


def rimmed_slope(field):
    return padded_2(field, (("band", 2),), 1)


def forward(current, hidden, memory, obs_weight, obs_target, weights):
    prior_in, prior_out, lstm_weight, lstm_bias, out_weight = weights
    units = out_weight.shape[1]
    state_wide = padded_2(current.astype(jnp.bfloat16), (("band", 2),), 2)
    state_rim = state_wide[:, :, 1:-1]
    pre_prior = conv_three(prior_in, state_wide)
    latent_rim = edge_zeroed(jax.nn.silu(pre_prior).astype(jnp.bfloat16))
    prior_state = conv_three(prior_out, latent_rim)
    cost_slope = obs_weight * current - obs_target + prior_weight * (current - prior_state)
    joined = jnp.concatenate([cost_slope, hidden], axis=1).astype(jnp.bfloat16)
    joined_rim = rimmed_field(joined)
    return lstm_tail(current, memory, state_rim, pre_prior, latent_rim, joined_rim, weights)

def forward_first(current, obs_weight, obs_target, weights):
    prior_in, prior_out, lstm_weight, lstm_bias, out_weight = weights
    units = out_weight.shape[1]
    frames = current.shape[1]
    batch, _, breadth, lat_count = current.shape
    fields = jnp.concatenate([current, obs_weight, obs_target], axis=1)
    wide = padded_2(fields, (("band", 2),), 3)
    current_wide = wide[:, :frames]
    state_wide = current_wide.astype(jnp.bfloat16)
    pre_wide = conv_three(prior_in, state_wide)
    latent_wide = edge_zeroed(jax.nn.silu(pre_wide).astype(jnp.bfloat16), 2)
    prior_state = conv_three(prior_out, latent_wide)
    near = wide[:, :, 2:-2]
    here, weight_near, target_near = near[:, :frames], near[:, frames : 2 * frames], near[:, 2 * frames :]
    cost_slope = weight_near * here - target_near + prior_weight * (here - prior_state)
    hidden_near = jnp.zeros((batch, units, breadth + 2, lat_count), jnp.float32)
    joined_rim = edge_zeroed(jnp.concatenate([cost_slope, hidden_near], axis=1).astype(jnp.bfloat16))
    memory = jnp.zeros((batch, units, breadth, lat_count), jnp.float32)
    state_rim = state_wide[:, :, 2:-2]
    pre_prior = pre_wide[:, :, 1:-1]
    latent_rim = latent_wide[:, :, 1:-1]
    return lstm_tail(current, memory, state_rim, pre_prior, latent_rim, joined_rim, weights)


def lstm_tail(current, memory, state_rim, pre_prior, latent_rim, joined_rim, weights):
    prior_in, prior_out, lstm_weight, lstm_bias, out_weight = weights
    units = out_weight.shape[1]
    gate_all = conv_three(lstm_weight, joined_rim, "io") + lstm_bias[None, :, None, None]
    in_gate = jax.nn.sigmoid(gate_all[:, :units])
    forget_gate = jax.nn.sigmoid(gate_all[:, units : 2 * units])
    out_gate = jax.nn.sigmoid(gate_all[:, 2 * units : 3 * units])
    update = jnp.tanh(gate_all[:, 3 * units :])
    memory_next = forget_gate * memory + in_gate * update
    squashed = jnp.tanh(memory_next)
    hidden_next = out_gate * squashed
    hidden_low = hidden_next.astype(jnp.bfloat16)
    stepped = jnp.einsum(
        "fh,bhwl->bfwl", out_weight, hidden_low, preferred_element_type=jnp.float32
    )
    saved = (
        state_rim,
        pre_prior,
        latent_rim,
        joined_rim,
        in_gate,
        forget_gate,
        out_gate,
        update,
        memory,
        squashed,
        hidden_low,
    )
    return (current - stepped, hidden_next, memory_next, saved)


def backward(slope_state, slope_hidden, slope_memory, saved, obs_weight, weights, leading):
    prior_in, prior_out, lstm_weight, lstm_bias, out_weight = weights
    (
        state_rim,
        pre_prior,
        latent_rim,
        joined_rim,
        in_gate,
        forget_gate,
        out_gate,
        update,
        memory,
        squashed,
        hidden_low,
    ) = saved
    frames = slope_state.shape[1]
    neg_low = (-slope_state).astype(jnp.bfloat16)
    grad_outw = jnp.einsum("bfwl,bhwl->fh", neg_low, hidden_low, preferred_element_type=jnp.float32)
    slope_hid = (
        jnp.einsum("fh,bfwl->bhwl", out_weight, neg_low, preferred_element_type=jnp.float32)
        + slope_hidden
    )
    slope_mem = slope_hid * out_gate * (1.0 - squashed * squashed) + slope_memory
    gate_slope = jnp.concatenate(
        [
            slope_mem * update * in_gate * (1.0 - in_gate),
            slope_mem * memory * forget_gate * (1.0 - forget_gate),
            slope_hid * squashed * out_gate * (1.0 - out_gate),
            slope_mem * in_gate * (1.0 - update * update),
        ],
        axis=1,
    )
    grad_bias = jnp.sum(gate_slope, axis=(0, 2, 3))
    gate_low = gate_slope.astype(jnp.bfloat16)
    grad_lstm = kernel_slope(gate_low, joined_rim, "io")
    back_kernel = lstm_weight[::-1]
    if leading:
        back_kernel = back_kernel[:, :frames]
    gate_rimmed = padded_2(gate_low, (("band", 2),), 1)
    joined_slope = conv_three(back_kernel, gate_rimmed)
    cost_part = joined_slope[:, :frames]
    hidden_back = None if leading else joined_slope[:, frames:]
    slope_prev = slope_state + (obs_weight + prior_weight) * cost_part
    prior_low = (-prior_weight * cost_part).astype(jnp.bfloat16)
    grad_pout = kernel_slope(prior_low, latent_rim)
    latent_slope = conv_three(flipped(prior_out), padded_2(prior_low, (("band", 2),), 2))
    sigma = jax.nn.sigmoid(pre_prior)
    pre_rim = (latent_slope * (sigma + pre_prior * sigma * (1.0 - sigma))).astype(jnp.bfloat16)
    pre_rim = edge_zeroed(pre_rim)
    grad_pin = kernel_slope(pre_rim[:, :, 1:-1], state_rim)
    slope_prev = slope_prev + conv_three(flipped(prior_in), pre_rim)
    memory_back = slope_mem * forget_gate
    return (
        slope_prev,
        hidden_back,
        memory_back,
        (grad_pin, grad_pout, grad_lstm, grad_bias, grad_outw),
    )


def body(
    first_guess,
    observed_height,
    swath_cells,
    drift_value,
    drift_cell,
    prior_in,
    prior_out,
    lstm_weight,
    lstm_bias,
    out_weight,
    final_slope,
):
    batch, frames, breadth, lat_count = first_guess.shape
    block = breadth * lat_count
    spots = jnp.arange(block, dtype=jnp.int32)
    hits = swath_cells[:, :, 0, :, None] == spots
    mask = jnp.any(hits, axis=2).astype(jnp.float32).reshape(batch, frames, breadth, lat_count)
    packed = jnp.stack([drift_value, drift_cell.astype(jnp.float32)])
    arrived = lax.all_to_all(packed, "band", split_axis=3, concat_axis=2, tiled=True)
    arrived_value = arrived[0].reshape(batch, -1)
    arrived_cell = arrived[1].astype(jnp.int32).reshape(batch, -1)
    places = jnp.arange(frames * block, dtype=jnp.int32).reshape(frames, breadth, lat_count)
    landed = arrived_cell[:, :, None, None, None] == places
    drift_count = jnp.sum(landed.astype(jnp.float32), axis=1)
    drift_total = jnp.sum(jnp.where(landed, arrived_value[:, :, None, None, None], 0.0), axis=1)
    obs_weight = mask + drift_count
    obs_target = mask * observed_height + drift_total
    weights = (prior_in, prior_out, lstm_weight, lstm_bias, out_weight)
    units = out_weight.shape[1]
    blank = jnp.zeros((batch, units, breadth, lat_count), jnp.float32)
    state_one, hid_one, mem_one, saved_one = forward_first(first_guess, obs_weight, obs_target, weights)
    state_two, hid_two, mem_two, saved_two = forward(
        state_one, hid_one, mem_one, obs_weight, obs_target, weights
    )
    slope_mid, hidden_back, memory_back, grads_two = backward(
        final_slope, blank, blank, saved_two, obs_weight, weights, False
    )
    slope_start, unused_hid, unused_mem, grads_one = backward(
        slope_mid, hidden_back, memory_back, saved_one, obs_weight, weights, True
    )
    summed = jax.tree.map(jnp.add, grads_one, grads_two)
    cells_all = batch * lax.axis_size("win") * breadth * lax.axis_size("band") * lat_count
    scale = 1.0 / jnp.sqrt(jnp.float32(cells_all))
    grad_pin, grad_pout, grad_lstm, grad_bias, grad_outw = summed
    taps, ins, outs = grad_lstm.shape
    rows = jnp.pad(grad_lstm, ((0, 0), (0, (-ins) % 8), (0, 0))).reshape(-1, outs)
    lstm_total = summed_everywhere(rows, "band", "win", jnp.bfloat16)
    lstm_total = lstm_total.reshape(taps, -1, outs)[:, :ins]
    small = [grad_pin, grad_pout, grad_bias, grad_outw]
    early = jnp.concatenate([member.reshape(-1) for member in small[1:]])
    early = summed_butterfly(early, "band", "win")
    late = summed_butterfly(grad_pin.reshape(-1), "band", "win")
    flat = jnp.concatenate([late, early])
    totals = []
    offset = 0
    for member in small:
        length = member.size
        totals.append(flat[offset : offset + length].reshape(member.shape))
        offset = offset + length
    totals = [totals[0], totals[1], lstm_total, totals[2], totals[3]]
    return (
        slope_start,
        totals[0] * scale,
        totals[1] * scale,
        totals[2] * scale,
        totals[3] * scale,
        totals[4] * scale,
    )


def summed_everywhere(flat, outer, inner, gathered=None):
    bands, wins = lax.axis_size(outer), lax.axis_size(inner)
    count = bands * wins
    if count & (count - 1):
        return lax.psum(flat, (outer, inner))
    axes = (outer, inner)
    inner_bits = wins.bit_length() - 1
    levels = (count.bit_length() - 1)
    order = ([inner_bits] if inner_bits < levels else []) + list(range(inner_bits)) + list(range(inner_bits + 1, levels))
    me = lax.axis_index(axes)
    extent = flat.shape[0]
    cur = jnp.pad(flat, [(0, (-extent) % count)] + [(0, 0)] * (flat.ndim - 1))
    for level in order:
        mask = 1 << level
        half = cur.shape[0] // 2
        high = (me & mask) != 0
        low_part, high_part = cur[:half], cur[half:]
        keep = jnp.where(high, high_part, low_part)
        send = jnp.where(high, low_part, high_part)
        cur = keep + lax.ppermute(send, axes, [(i, i ^ mask) for i in range(count)])
    total_type = cur.dtype
    if gathered is not None:
        cur = cur.astype(gathered)
    for level in reversed(order):
        mask = 1 << level
        high = (me & mask) != 0
        other = lax.ppermute(cur, axes, [(i, i ^ mask) for i in range(count)])
        cur = jnp.where(high, jnp.concatenate([other, cur]), jnp.concatenate([cur, other]))
    return cur[:extent].astype(total_type)


def summed_butterfly(flat, outer, inner):
    bands, wins = lax.axis_size(outer), lax.axis_size(inner)
    count = bands * wins
    if count & (count - 1):
        return lax.psum(flat, (outer, inner))
    axes = (outer, inner)
    inner_bits = wins.bit_length() - 1
    levels = count.bit_length() - 1
    order = ([inner_bits] if inner_bits < levels else []) + list(range(inner_bits)) + list(range(inner_bits + 1, levels))
    for level in order:
        mask = 1 << level
        flat = flat + lax.ppermute(flat, axes, [(i, i ^ mask) for i in range(count)])
    return flat


def solution(mesh):
    return jax.shard_map(
        body,
        mesh=mesh,
        in_specs=(
            P("win", None, "band", None),
            P("win", None, "band", None),
            P("win", None, "band", None),
            P("win", "band", None, None),
            P("win", "band", None, None),
            P(),
            P(),
            P(),
            P(),
            P(),
            P("win", None, "band", None),
        ),
        out_specs=(P("win", None, "band", None), P(), P(), P(), P(), P()),
        check_vma=False,
    )
```
